256 devices in a mesh: seg: 32 (over x, z_hi, core), band: 8 (over y, z_lo).
Axes of the slice: x: 4, y: 4, z: 8 (z_hi: 4, z_lo: 2; z = z_hi * 2 + z_lo), core: 2. Of those that a mesh axis runs over, the one named last changes fastest.
Arguments:
- spectra: bfloat16 [2, 32768, 1024], P(None, 'seg', 'band'), may hold values from -100 to 100, as said below
- pair_first: int32 [131072], P('seg'), may hold values from 0 to 32767, as said below
- pair_second: int32 [131072], P('seg'), may hold values from 0 to 32767, as said below
- pair_bin: int32 [131072], P('seg'), may hold values from 0 to 255, as said below
Outputs:
- correlation_stack: float32 [256, 1024], P('seg', 'band')
The draws below stay inside these ranges and needn't reach their ends.
Inputs may be any that keep to these rules, and one draw needn't show every extreme that they name: The spectra are finite; their magnitude varies from channel to channel and from bin to bin. `pair_first`: rows s * 4096 to (s + 1) * 4096 - 1 name channels of segment s, that is s * 1024 to (s + 1) * 1024 - 1. pair_second differs from pair_first of the same row by 1 to 256 in either direction; some row of every segment differs by exactly 256. `pair_bin`: offset bins s * 8 to (s + 1) * 8 - 1 belong to segment s; of one segment's rows at most 256 have bins of any one segment, and in every draw the bins of some segment receive exactly 256 rows from every segment.
All inputs are finite; a program needn't handle non-finite values.
Results may differ from the reference program's by a relative error of at most 0.0054.
Values may be sent and summed in bfloat16 or wider, within the bound.
No kernel may reach another device: no remote copies, remote signals or barrier semaphores. Data moves between devices by JAX's collectives and lax.ppermute only.
A program may use at most 64 MiB of HBM per device.

```python
import math
import jax
import jax.numpy as jnp
from jax import lax

CH_DEV = 1024
PAIRS_DEV = 4096
OB_DEV = 8
REACH = 256
FREQ = 1024
LAGS = 1024
HALF_WIN = 64
CAP = 256
CHANNELS = 32768
NPAIRS = 131072
OBINS = 256
N_SEG = 32


def draw_spectra(key, part):
    bins_frac = jnp.arange(FREQ, dtype=jnp.float32)[None, :] / FREQ
    amplitude = jax.random.uniform(jax.random.fold_in(key, 1), (CHANNELS, 1), minval=0.5, maxval=1.2)
    cycles = jax.random.uniform(jax.random.fold_in(key, 2), (CHANNELS, 1), minval=1.0, maxval=3.0)
    offset_phase = jax.random.uniform(jax.random.fold_in(key, 3), (CHANNELS, 1), minval=0.0, maxval=6.283)
    envelope = jnp.exp(amplitude * jnp.sin(6.2832 * cycles * bins_frac + offset_phase))
    roughness = jnp.exp(jax.random.uniform(jax.random.fold_in(key, 4), (CHANNELS, FREQ), maxval=math.log(3.0)))
    noise_part = jax.random.truncated_normal(jax.random.fold_in(key, 5), -4.0, 4.0, (2, CHANNELS, FREQ))
    values = noise_part * (envelope * roughness)[None]
    return values.astype(jnp.bfloat16)


def pair_channels(key):
    row_index = jnp.arange(NPAIRS, dtype=jnp.int32)
    segment_of = row_index // PAIRS_DEV
    within = jax.random.randint(jax.random.fold_in(key, 11), (NPAIRS,), 0, CH_DEV)
    firsts = segment_of * CH_DEV + within
    distance = jax.random.randint(jax.random.fold_in(key, 12), (NPAIRS,), 1, REACH + 1)
    distance = jnp.where(row_index % PAIRS_DEV == 0, REACH, distance)
    direction = 2 * jax.random.randint(jax.random.fold_in(key, 13), (NPAIRS,), 0, 2) - 1
    seconds = firsts + direction * distance
    outside = (seconds < 0) | (seconds >= CHANNELS)
    seconds = jnp.where(outside, firsts - direction * distance, seconds)
    return (firsts.astype(jnp.int32), seconds.astype(jnp.int32))


def draw_pair_first(key, part):
    return pair_channels(key)[0]


def draw_pair_second(key, part):
    return pair_channels(key)[1]


def draw_pair_bin(key, part):
    segments = NPAIRS // PAIRS_DEV
    hottest = jax.random.randint(jax.random.fold_in(key, 21), (), 0, segments)
    row_rank = jnp.arange(PAIRS_DEV, dtype=jnp.int32)
    spread_owner = (hottest + 1 + (row_rank - CAP) % (segments - 1)) % segments
    owner_list = jnp.where(row_rank < CAP, hottest, spread_owner)

    def one_block(block_key):
        return owner_list[jax.random.permutation(block_key, PAIRS_DEV)]
    block_keys = jax.random.split(jax.random.fold_in(key, 22), segments)
    owners_all = jax.vmap(one_block)(block_keys).reshape(-1)
    local_bin = jax.random.randint(jax.random.fold_in(key, 23), (NPAIRS,), 0, OB_DEV)
    return (owners_all * OB_DEV + local_bin).astype(jnp.int32)


def setup_inputs(seed: int = 0) -> dict:
    seeds = jax.random.split(jax.random.key(seed), 5)
    return {
        "spectra": draw_spectra(jax.random.fold_in(seeds[4], 71), 0),
        "pair_first": draw_pair_first(jax.random.fold_in(seeds[4], 71), 0),
        "pair_second": draw_pair_second(jax.random.fold_in(seeds[4], 71), 0),
        "pair_bin": draw_pair_bin(jax.random.fold_in(seeds[4], 71), 0),
    }


epsilon = 1e-06

def lag_table(first_bin, local_bins, total_bins, lag_count):
    frequency = first_bin + jnp.arange(local_bins, dtype=jnp.int32)
    lag_index = jnp.arange(lag_count, dtype=jnp.int32) - lag_count // 2
    residue = frequency[:, None] * lag_index[None, :] % (2 * total_bins)
    angles = residue.astype(jnp.float32) * (math.pi / total_bins)
    cosine = jnp.cos(angles) / total_bins
    negsine = -jnp.sin(angles) / total_bins
    return jnp.concatenate([cosine, negsine], axis=0).astype(jnp.bfloat16)

def reference(spectra, pair_first, pair_second, pair_bin):
    real_part = spectra[0].astype(jnp.float32)
    imag_part = spectra[1].astype(jnp.float32)
    power_sum = real_part * real_part + imag_part * imag_part
    window_sum = lax.reduce_window(power_sum, jnp.zeros((), power_sum.dtype), lax.add, (1, 2 * HALF_WIN + 1), (1, 1), ((0, 0), (HALF_WIN, HALF_WIN)))
    scaling = lax.rsqrt(window_sum / (2 * HALF_WIN + 1) + epsilon)
    white_real = (real_part * scaling).astype(jnp.bfloat16)
    white_imag = (imag_part * scaling).astype(jnp.bfloat16)
    table = lag_table(0, FREQ, FREQ, LAGS).astype(jnp.float32)

    def add_block(running, block_data):
        firsts, seconds, bin_ids = block_data
        first_real = white_real[firsts].astype(jnp.float32)
        first_imag = white_imag[firsts].astype(jnp.float32)
        second_real = white_real[seconds].astype(jnp.float32)
        second_imag = white_imag[seconds].astype(jnp.float32)
        cross_real = first_real * second_real + first_imag * second_imag
        cross_imag = first_imag * second_real - first_real * second_imag
        cross_both = jnp.concatenate([cross_real, cross_imag], axis=1).astype(jnp.bfloat16)
        cross_both = lax.optimization_barrier(cross_both).astype(jnp.float32)
        return (running + jax.ops.segment_sum(cross_both, bin_ids, num_segments=OBINS), None)
    blocks = (pair_first.reshape(N_SEG, PAIRS_DEV), pair_second.reshape(N_SEG, PAIRS_DEV), pair_bin.reshape(N_SEG, PAIRS_DEV))
    stacked, _ = lax.scan(add_block, jnp.zeros((OBINS, 2 * FREQ), jnp.float32), blocks)
    return jnp.dot(stacked, table, precision=lax.Precision.HIGHEST)
```

```python
import math

import jax
import jax.numpy as jnp
from jax import lax
from jax.sharding import PartitionSpec as P

OB_DEV = 8
REACH = 256
FREQ = 1024
LAGS = 1024
HALF_WIN = 64


epsilon = 1e-06


def extended(block, sides, width):
    for axis, dim in sides:
        count = lax.axis_size(axis)
        forward = [(i, i + 1) for i in range(count - 1)]
        backward = [(target, source) for source, target in forward]
        low = lax.ppermute(
            lax.slice_in_dim(block, block.shape[dim] - width, None, axis=dim), axis, forward
        )
        high = lax.ppermute(lax.slice_in_dim(block, 0, width, axis=dim), axis, backward)
        block = jnp.concatenate([low, block, high], axis=dim)
    return block


def window_matrix(local_bins, half_width):
    padded_index = jnp.arange(local_bins + 2 * half_width)[:, None]
    bin_index = jnp.arange(local_bins)[None, :]
    inside = (padded_index >= bin_index) & (padded_index <= bin_index + 2 * half_width)
    return inside.astype(jnp.bfloat16)


def exact_dot(values, selector):
    high = values.astype(jnp.bfloat16)
    rest = values - high.astype(jnp.float32)
    mid = rest.astype(jnp.bfloat16)
    low = (rest - mid.astype(jnp.float32)).astype(jnp.bfloat16)
    total = jnp.dot(high, selector, preferred_element_type=jnp.float32)
    total = total + jnp.dot(mid, selector, preferred_element_type=jnp.float32)
    return total + jnp.dot(low, selector, preferred_element_type=jnp.float32)


def lag_table(first_bin, local_bins, total_bins, lag_count):
    frequency = first_bin + jnp.arange(local_bins, dtype=jnp.int32)
    lag_index = jnp.arange(lag_count, dtype=jnp.int32) - lag_count // 2
    residue = frequency[:, None] * lag_index[None, :] % (2 * total_bins)
    angles = residue.astype(jnp.float32) * (math.pi / total_bins)
    cosine = jnp.cos(angles) / total_bins
    negsine = -jnp.sin(angles) / total_bins
    return jnp.concatenate([cosine, negsine], axis=0).astype(jnp.bfloat16)


def per_device(spectra, pair_first, pair_second, pair_bin):
    seg_position = lax.axis_index("seg")
    band_position = lax.axis_index("band")
    segments = lax.axis_size("seg")
    bands = lax.axis_size("band")
    channels = spectra.shape[1]
    local_bins = spectra.shape[2]
    real_part = spectra[0].astype(jnp.float32)
    imag_part = spectra[1].astype(jnp.float32)
    power_sum = real_part * real_part + imag_part * imag_part
    padded_power = extended(power_sum, (("band", 1),), HALF_WIN)
    window_sum = exact_dot(padded_power, window_matrix(local_bins, HALF_WIN))
    scaling = lax.rsqrt(window_sum / (2 * HALF_WIN + 1) + epsilon)
    whitened = jnp.concatenate([real_part * scaling, imag_part * scaling], axis=1).astype(
        jnp.bfloat16
    )
    first_rows = whitened[pair_first - seg_position * channels]
    near_rows = extended(whitened, (("seg", 0),), REACH)
    second_rows = near_rows[pair_second - seg_position * channels + REACH]
    first_real = first_rows[:, :local_bins].astype(jnp.float32)
    first_imag = first_rows[:, local_bins:].astype(jnp.float32)
    second_real = second_rows[:, :local_bins].astype(jnp.float32)
    second_imag = second_rows[:, local_bins:].astype(jnp.float32)
    cross_real = first_real * second_real + first_imag * second_imag
    cross_imag = first_imag * second_real - first_real * second_imag
    cross_both = jnp.concatenate([cross_real, cross_imag], axis=1).astype(jnp.bfloat16)
    all_bins = segments * OB_DEV
    members = (pair_bin[:, None] == jnp.arange(all_bins, dtype=jnp.int32)[None, :]).astype(
        jnp.bfloat16
    )
    local_stack = lax.dot_general(
        members, cross_both, (((0,), (0,)), ((), ())), preferred_element_type=jnp.float32
    )
    gathered = lax.all_to_all(local_stack, "seg", split_axis=0, concat_axis=0, tiled=True)
    stack = jnp.sum(gathered.reshape(segments, OB_DEV, 2 * local_bins), axis=0)
    table = lag_table(band_position * local_bins, local_bins, FREQ, LAGS)
    partial_lags = jnp.dot(
        stack, table.astype(jnp.float32), precision=lax.Precision.HIGHEST
    )
    pieces = lax.all_to_all(partial_lags, "band", split_axis=1, concat_axis=0, tiled=True)
    return jnp.sum(pieces.reshape(bands, OB_DEV, LAGS // bands), axis=0)


def solution(mesh):
    placed = (P(None, "seg", "band"), P("seg"), P("seg"), P("seg"))
    return jax.shard_map(
        per_device, mesh=mesh, in_specs=placed, out_specs=P("seg", "band"), check_vma=False
    )
```

```python
import math

import jax
import jax.numpy as jnp
from jax import lax
from jax.sharding import PartitionSpec as P

OB_DEV = 8
REACH = 256
FREQ = 1024
LAGS = 1024
HALF_WIN = 64


epsilon = 1e-06


def extended(block, sides, width):
    for axis, dim in sides:
        count = lax.axis_size(axis)
        forward = [(i, i + 1) for i in range(count - 1)]
        backward = [(target, source) for source, target in forward]
        low = lax.ppermute(
            lax.slice_in_dim(block, block.shape[dim] - width, None, axis=dim), axis, forward
        )
        high = lax.ppermute(lax.slice_in_dim(block, 0, width, axis=dim), axis, backward)
        block = jnp.concatenate([low, block, high], axis=dim)
    return block


def window_matrix(local_bins, half_width):
    padded_index = jnp.arange(local_bins + 2 * half_width)[:, None]
    bin_index = jnp.arange(local_bins)[None, :]
    inside = (padded_index >= bin_index) & (padded_index <= bin_index + 2 * half_width)
    return inside.astype(jnp.bfloat16)


def exact_dot(values, selector):
    high = lax.reduce_precision(values, exponent_bits=8, mantissa_bits=7)
    rest = values - high
    mid = lax.reduce_precision(rest, exponent_bits=8, mantissa_bits=7)
    low = rest - mid
    total = jnp.dot(high.astype(jnp.bfloat16), selector, preferred_element_type=jnp.float32)
    total = total + jnp.dot(mid.astype(jnp.bfloat16), selector, preferred_element_type=jnp.float32)
    return total + jnp.dot(low.astype(jnp.bfloat16), selector, preferred_element_type=jnp.float32)


def select_rows(table, index):
    chosen = (index[:, None] == jnp.arange(table.shape[0], dtype=jnp.int32)[None, :]).astype(
        table.dtype
    )
    return jnp.dot(chosen, table, preferred_element_type=jnp.float32)


def lag_table(first_bin, local_bins, total_bins, lag_count):
    frequency = first_bin + jnp.arange(local_bins, dtype=jnp.int32)
    lag_index = jnp.arange(lag_count, dtype=jnp.int32) - lag_count // 2
    residue = frequency[:, None] * lag_index[None, :] % (2 * total_bins)
    angles = residue.astype(jnp.float32) * (math.pi / total_bins)
    cosine = jnp.cos(angles) / total_bins
    negsine = -jnp.sin(angles) / total_bins
    return jnp.concatenate([cosine, negsine], axis=0).astype(jnp.bfloat16)


def per_device(spectra, pair_first, pair_second, pair_bin):
    seg_position = lax.axis_index("seg")
    band_position = lax.axis_index("band")
    segments = lax.axis_size("seg")
    bands = lax.axis_size("band")
    channels = spectra.shape[1]
    local_bins = spectra.shape[2]
    real_part = spectra[0].astype(jnp.float32)
    imag_part = spectra[1].astype(jnp.float32)
    power_sum = real_part * real_part + imag_part * imag_part
    padded_power = extended(power_sum, (("band", 1),), HALF_WIN)
    window_sum = exact_dot(padded_power, window_matrix(local_bins, HALF_WIN))
    scaling = lax.rsqrt(window_sum / (2 * HALF_WIN + 1) + epsilon)
    whitened = jnp.concatenate([real_part * scaling, imag_part * scaling], axis=1).astype(
        jnp.bfloat16
    )
    first_rows = select_rows(whitened, pair_first - seg_position * channels)
    near_rows = extended(whitened, (("seg", 0),), REACH)
    second_rows = select_rows(near_rows, pair_second - seg_position * channels + REACH)
    first_real = first_rows[:, :local_bins]
    first_imag = first_rows[:, local_bins:]
    second_real = second_rows[:, :local_bins]
    second_imag = second_rows[:, local_bins:]
    cross_real = first_real * second_real + first_imag * second_imag
    cross_imag = first_imag * second_real - first_real * second_imag
    cross_both = jnp.concatenate([cross_real, cross_imag], axis=1).astype(jnp.bfloat16)
    all_bins = segments * OB_DEV
    members = (pair_bin[:, None] == jnp.arange(all_bins, dtype=jnp.int32)[None, :]).astype(
        jnp.bfloat16
    )
    local_stack = lax.dot_general(
        members, cross_both, (((0,), (0,)), ((), ())), preferred_element_type=jnp.float32
    )
    gathered = lax.all_to_all(local_stack, "seg", split_axis=0, concat_axis=0, tiled=True)
    stack = jnp.sum(gathered.reshape(segments, OB_DEV, 2 * local_bins), axis=0)
    table = lag_table(band_position * local_bins, local_bins, FREQ, LAGS)
    partial_lags = jnp.dot(
        stack, table.astype(jnp.float32), precision=lax.Precision.HIGHEST
    )
    pieces = lax.all_to_all(partial_lags, "band", split_axis=1, concat_axis=0, tiled=True)
    return jnp.sum(pieces.reshape(bands, OB_DEV, LAGS // bands), axis=0)


def solution(mesh):
    placed = (P(None, "seg", "band"), P("seg"), P("seg"), P("seg"))
    return jax.shard_map(
        per_device, mesh=mesh, in_specs=placed, out_specs=P("seg", "band"), check_vma=False
    )
```

```python
import math

import jax
import jax.numpy as jnp
from jax import lax
from jax.sharding import PartitionSpec as P

OB_DEV = 8
REACH = 256
FREQ = 1024
LAGS = 1024
HALF_WIN = 64


epsilon = 1e-06


def extended(block, sides, width):
    for axis, dim in sides:
        count = lax.axis_size(axis)
        forward = [(i, i + 1) for i in range(count - 1)]
        backward = [(target, source) for source, target in forward]
        low = lax.ppermute(
            lax.slice_in_dim(block, block.shape[dim] - width, None, axis=dim), axis, forward
        )
        high = lax.ppermute(lax.slice_in_dim(block, 0, width, axis=dim), axis, backward)
        block = jnp.concatenate([low, block, high], axis=dim)
    return block


def window_matrix(local_bins, half_width):
    padded_index = jnp.arange(local_bins + 2 * half_width)[:, None]
    bin_index = jnp.arange(local_bins)[None, :]
    inside = (padded_index >= bin_index) & (padded_index <= bin_index + 2 * half_width)
    return inside.astype(jnp.bfloat16)


def exact_dot(values, selector):
    high = lax.reduce_precision(values, exponent_bits=8, mantissa_bits=7)
    rest = values - high
    mid = lax.reduce_precision(rest, exponent_bits=8, mantissa_bits=7)
    low = rest - mid
    total = jnp.dot(high.astype(jnp.bfloat16), selector, preferred_element_type=jnp.float32)
    total = total + jnp.dot(mid.astype(jnp.bfloat16), selector, preferred_element_type=jnp.float32)
    return total + jnp.dot(low.astype(jnp.bfloat16), selector, preferred_element_type=jnp.float32)


def select_rows(table, index):
    chosen = (index[:, None] == jnp.arange(table.shape[0], dtype=jnp.int32)[None, :]).astype(
        table.dtype
    )
    return jnp.dot(chosen, table, preferred_element_type=jnp.float32)


def lag_table(first_bin, local_bins, total_bins, lag_count):
    frequency = first_bin + jnp.arange(local_bins, dtype=jnp.int32)
    lag_index = jnp.arange(lag_count, dtype=jnp.int32) - lag_count // 2
    residue = frequency[:, None] * lag_index[None, :] % (2 * total_bins)
    angles = residue.astype(jnp.float32) * (math.pi / total_bins)
    cosine = jnp.cos(angles) / total_bins
    negsine = -jnp.sin(angles) / total_bins
    return jnp.concatenate([cosine, negsine], axis=0).astype(jnp.bfloat16)


def per_device(spectra, pair_first, pair_second, pair_bin):
    seg_position = lax.axis_index("seg")
    band_position = lax.axis_index("band")
    segments = lax.axis_size("seg")
    bands = lax.axis_size("band")
    channels = spectra.shape[1]
    local_bins = spectra.shape[2]
    real_part = spectra[0].astype(jnp.float32)
    imag_part = spectra[1].astype(jnp.float32)
    power_sum = real_part * real_part + imag_part * imag_part
    padded_power = extended(power_sum, (("band", 1),), HALF_WIN)
    window_sum = exact_dot(padded_power, window_matrix(local_bins, HALF_WIN))
    scaling = lax.rsqrt(window_sum / (2 * HALF_WIN + 1) + epsilon)
    whitened = jnp.concatenate([real_part * scaling, imag_part * scaling], axis=1).astype(
        jnp.bfloat16
    )
    first_rows = select_rows(whitened, pair_first - seg_position * channels)
    near_rows = extended(whitened, (("seg", 0),), REACH)
    second_rows = select_rows(near_rows, pair_second - seg_position * channels + REACH)
    first_real = first_rows[:, :local_bins]
    first_imag = first_rows[:, local_bins:]
    second_real = second_rows[:, :local_bins]
    second_imag = second_rows[:, local_bins:]
    cross_real = first_real * second_real + first_imag * second_imag
    cross_imag = first_imag * second_real - first_real * second_imag
    cross_both = jnp.concatenate([cross_real, cross_imag], axis=1).astype(jnp.bfloat16)
    all_bins = segments * OB_DEV
    members = (pair_bin[:, None] == jnp.arange(all_bins, dtype=jnp.int32)[None, :]).astype(
        jnp.bfloat16
    )
    local_stack = lax.dot_general(
        members, cross_both, (((0,), (0,)), ((), ())), preferred_element_type=jnp.float32
    )
    gathered = lax.all_to_all(
        local_stack.astype(jnp.bfloat16), "seg", split_axis=0, concat_axis=0, tiled=True
    )
    stack = jnp.sum(
        gathered.reshape(segments, OB_DEV, 2 * local_bins).astype(jnp.float32), axis=0
    )
    table = lag_table(band_position * local_bins, local_bins, FREQ, LAGS)
    partial_lags = jnp.dot(
        stack, table.astype(jnp.float32), precision=lax.Precision.HIGHEST
    )
    pieces = lax.all_to_all(partial_lags, "band", split_axis=1, concat_axis=0, tiled=True)
    return jnp.sum(pieces.reshape(bands, OB_DEV, LAGS // bands), axis=0)


def solution(mesh):
    placed = (P(None, "seg", "band"), P("seg"), P("seg"), P("seg"))
    return jax.shard_map(
        per_device, mesh=mesh, in_specs=placed, out_specs=P("seg", "band"), check_vma=False
    )
```

```python
import math

import jax
import jax.numpy as jnp
from jax import lax
from jax.sharding import PartitionSpec as P

OB_DEV = 8
REACH = 256
FREQ = 1024
LAGS = 1024
HALF_WIN = 64


epsilon = 1e-06


def extended(block, sides, width):
    for axis, dim in sides:
        count = lax.axis_size(axis)
        forward = [(i, i + 1) for i in range(count - 1)]
        backward = [(target, source) for source, target in forward]
        low = lax.ppermute(
            lax.slice_in_dim(block, block.shape[dim] - width, None, axis=dim), axis, forward
        )
        high = lax.ppermute(lax.slice_in_dim(block, 0, width, axis=dim), axis, backward)
        block = jnp.concatenate([low, block, high], axis=dim)
    return block


def halos(block, axis, width):
    count = lax.axis_size(axis)
    forward = [(i, i + 1) for i in range(count - 1)]
    backward = [(target, source) for source, target in forward]
    low = lax.ppermute(block[block.shape[0] - width :], axis, forward)
    high = lax.ppermute(block[:width], axis, backward)
    return low, high


def window_matrix(local_bins, half_width):
    padded_index = jnp.arange(local_bins + 2 * half_width)[:, None]
    bin_index = jnp.arange(local_bins)[None, :]
    inside = (padded_index >= bin_index) & (padded_index <= bin_index + 2 * half_width)
    return inside.astype(jnp.bfloat16)


def exact_dot(values, selector):
    high = lax.reduce_precision(values, exponent_bits=8, mantissa_bits=7)
    rest = values - high
    mid = lax.reduce_precision(rest, exponent_bits=8, mantissa_bits=7)
    low = rest - mid
    total = jnp.dot(high.astype(jnp.bfloat16), selector, preferred_element_type=jnp.float32)
    total = total + jnp.dot(mid.astype(jnp.bfloat16), selector, preferred_element_type=jnp.float32)
    return total + jnp.dot(low.astype(jnp.bfloat16), selector, preferred_element_type=jnp.float32)


def select_rows(table, index):
    chosen = (index[:, None] == jnp.arange(table.shape[0], dtype=jnp.int32)[None, :]).astype(
        table.dtype
    )
    return jnp.dot(chosen, table, preferred_element_type=jnp.float32)


def lag_table(first_bin, local_bins, total_bins, lag_count):
    frequency = first_bin + jnp.arange(local_bins, dtype=jnp.int32)
    lag_index = jnp.arange(lag_count, dtype=jnp.int32) - lag_count // 2
    residue = frequency[:, None] * lag_index[None, :] % (2 * total_bins)
    angles = residue.astype(jnp.float32) * (math.pi / total_bins)
    cosine = jnp.cos(angles) / total_bins
    negsine = -jnp.sin(angles) / total_bins
    return jnp.concatenate([cosine, negsine], axis=0).astype(jnp.bfloat16)


def per_device(spectra, pair_first, pair_second, pair_bin):
    seg_position = lax.axis_index("seg")
    band_position = lax.axis_index("band")
    segments = lax.axis_size("seg")
    bands = lax.axis_size("band")
    channels = spectra.shape[1]
    local_bins = spectra.shape[2]
    real_part = spectra[0].astype(jnp.float32)
    imag_part = spectra[1].astype(jnp.float32)
    power_sum = real_part * real_part + imag_part * imag_part
    padded_power = extended(power_sum, (("band", 1),), HALF_WIN)
    window_sum = exact_dot(padded_power, window_matrix(local_bins, HALF_WIN))
    scaling = lax.rsqrt(window_sum / (2 * HALF_WIN + 1) + epsilon)
    whitened = jnp.concatenate([real_part * scaling, imag_part * scaling], axis=1).astype(
        jnp.bfloat16
    )
    first_rows = select_rows(whitened, pair_first - seg_position * channels)
    low_rows, high_rows = halos(whitened, "seg", REACH)
    second_local = pair_second - seg_position * channels
    second_rows = select_rows(whitened, second_local)
    second_rows = second_rows + select_rows(low_rows, second_local + REACH)
    second_rows = second_rows + select_rows(high_rows, second_local - channels)
    first_real = first_rows[:, :local_bins]
    first_imag = first_rows[:, local_bins:]
    second_real = second_rows[:, :local_bins]
    second_imag = second_rows[:, local_bins:]
    cross_real = first_real * second_real + first_imag * second_imag
    cross_imag = first_imag * second_real - first_real * second_imag
    cross_both = jnp.concatenate([cross_real, cross_imag], axis=1).astype(jnp.bfloat16)
    all_bins = segments * OB_DEV
    members = (pair_bin[:, None] == jnp.arange(all_bins, dtype=jnp.int32)[None, :]).astype(
        jnp.bfloat16
    )
    local_stack = lax.dot_general(
        members, cross_both, (((0,), (0,)), ((), ())), preferred_element_type=jnp.float32
    )
    gathered = lax.all_to_all(local_stack, "seg", split_axis=0, concat_axis=0, tiled=True)
    stack = jnp.sum(gathered.reshape(segments, OB_DEV, 2 * local_bins), axis=0)
    table = lag_table(band_position * local_bins, local_bins, FREQ, LAGS)
    partial_lags = jnp.dot(
        stack, table.astype(jnp.float32), precision=lax.Precision.HIGHEST
    )
    pieces = lax.all_to_all(partial_lags, "band", split_axis=1, concat_axis=0, tiled=True)
    return jnp.sum(pieces.reshape(bands, OB_DEV, LAGS // bands), axis=0)


def solution(mesh):
    placed = (P(None, "seg", "band"), P("seg"), P("seg"), P("seg"))
    return jax.shard_map(
        per_device, mesh=mesh, in_specs=placed, out_specs=P("seg", "band"), check_vma=False
    )
```

```python
import math

import jax
import jax.numpy as jnp
from jax import lax
from jax.sharding import PartitionSpec as P

OB_DEV = 8
REACH = 256
FREQ = 1024
LAGS = 1024
HALF_WIN = 64


epsilon = 1e-06


def extended(block, sides, width):
    for axis, dim in sides:
        count = lax.axis_size(axis)
        forward = [(i, i + 1) for i in range(count - 1)]
        backward = [(target, source) for source, target in forward]
        low = lax.ppermute(
            lax.slice_in_dim(block, block.shape[dim] - width, None, axis=dim), axis, forward
        )
        high = lax.ppermute(lax.slice_in_dim(block, 0, width, axis=dim), axis, backward)
        block = jnp.concatenate([low, block, high], axis=dim)
    return block


def window_matrix(local_bins, half_width):
    padded_index = jnp.arange(local_bins + 2 * half_width)[:, None]
    bin_index = jnp.arange(local_bins)[None, :]
    inside = (padded_index >= bin_index) & (padded_index <= bin_index + 2 * half_width)
    return inside.astype(jnp.bfloat16)


def exact_dot(values, selector):
    high = lax.reduce_precision(values, exponent_bits=8, mantissa_bits=7)
    rest = values - high
    mid = lax.reduce_precision(rest, exponent_bits=8, mantissa_bits=7)
    low = rest - mid
    total = jnp.dot(high.astype(jnp.bfloat16), selector, preferred_element_type=jnp.float32)
    total = total + jnp.dot(mid.astype(jnp.bfloat16), selector, preferred_element_type=jnp.float32)
    return total + jnp.dot(low.astype(jnp.bfloat16), selector, preferred_element_type=jnp.float32)


def select_rows(table, index):
    chosen = (index[:, None] == jnp.arange(table.shape[0], dtype=jnp.int32)[None, :]).astype(
        table.dtype
    )
    return jnp.dot(chosen, table, preferred_element_type=jnp.float32)


def lag_table(first_bin, local_bins, total_bins, lag_count):
    frequency = first_bin + jnp.arange(local_bins, dtype=jnp.int32)
    lag_index = jnp.arange(lag_count, dtype=jnp.int32) - lag_count // 2
    residue = frequency[:, None] * lag_index[None, :] % (2 * total_bins)
    angles = residue.astype(jnp.float32) * (math.pi / total_bins)
    cosine = jnp.cos(angles) / total_bins
    negsine = -jnp.sin(angles) / total_bins
    return jnp.concatenate([cosine, negsine], axis=0).astype(jnp.bfloat16)


def shifted(block, axes, steps):
    sizes = [lax.axis_size(axis) for axis in axes]
    pairs = []
    for source in range(math.prod(sizes)):
        coords = []
        rest = source
        for size in reversed(sizes):
            coords.append(rest % size)
            rest //= size
        coords = coords[::-1]
        target = [c + d for c, d in zip(coords, steps)]
        if all(0 <= t < size for t, size in zip(target, sizes)):
            flat = 0
            for t, size in zip(target, sizes):
                flat = flat * size + t
            pairs.append((source, flat))
    return lax.ppermute(block, axes if len(axes) > 1 else axes[0], pairs)


def per_device(spectra, pair_first, pair_second, pair_bin):
    seg_position = lax.axis_index("seg")
    band_position = lax.axis_index("band")
    segments = lax.axis_size("seg")
    bands = lax.axis_size("band")
    channels = spectra.shape[1]
    local_bins = spectra.shape[2]
    both = ("seg", "band")
    low_spectra = shifted(spectra[:, channels - REACH :], ("seg",), (1,))
    high_spectra = shifted(spectra[:, :REACH], ("seg",), (-1,))
    near_spectra = jnp.concatenate([low_spectra, spectra, high_spectra], axis=1).astype(jnp.float32)
    real_part = near_spectra[0]
    imag_part = near_spectra[1]
    own = spectra.astype(jnp.float32)
    own_power = own[0] * own[0] + own[1] * own[1]
    left = shifted(own_power[:, local_bins - HALF_WIN :], ("band",), (1,))
    right = shifted(own_power[:, :HALF_WIN], ("band",), (-1,))
    corner_ll = shifted(own_power[channels - REACH :, local_bins - HALF_WIN :], both, (1, 1))
    corner_lr = shifted(own_power[channels - REACH :, :HALF_WIN], both, (1, -1))
    corner_hl = shifted(own_power[:REACH, local_bins - HALF_WIN :], both, (-1, 1))
    corner_hr = shifted(own_power[:REACH, :HALF_WIN], both, (-1, -1))
    power_sum = real_part * real_part + imag_part * imag_part
    padded_power = jnp.concatenate(
        [
            jnp.concatenate([corner_ll, left, corner_hl], axis=0),
            power_sum,
            jnp.concatenate([corner_lr, right, corner_hr], axis=0),
        ],
        axis=1,
    )
    window_sum = exact_dot(padded_power, window_matrix(local_bins, HALF_WIN))
    scaling = lax.rsqrt(window_sum / (2 * HALF_WIN + 1) + epsilon)
    near_rows = jnp.concatenate([real_part * scaling, imag_part * scaling], axis=1).astype(
        jnp.bfloat16
    )
    first_rows = select_rows(near_rows[REACH : REACH + channels], pair_first - seg_position * channels)
    second_rows = select_rows(near_rows, pair_second - seg_position * channels + REACH)
    first_real = first_rows[:, :local_bins]
    first_imag = first_rows[:, local_bins:]
    second_real = second_rows[:, :local_bins]
    second_imag = second_rows[:, local_bins:]
    cross_real = first_real * second_real + first_imag * second_imag
    cross_imag = first_imag * second_real - first_real * second_imag
    cross_both = jnp.concatenate([cross_real, cross_imag], axis=1).astype(jnp.bfloat16)
    all_bins = segments * OB_DEV
    members = (pair_bin[:, None] == jnp.arange(all_bins, dtype=jnp.int32)[None, :]).astype(
        jnp.bfloat16
    )
    local_stack = lax.dot_general(
        members, cross_both, (((0,), (0,)), ((), ())), preferred_element_type=jnp.float32
    )
    gathered = lax.all_to_all(local_stack, "seg", split_axis=0, concat_axis=0, tiled=True)
    stack = jnp.sum(gathered.reshape(segments, OB_DEV, 2 * local_bins), axis=0)
    table = lag_table(band_position * local_bins, local_bins, FREQ, LAGS)
    partial_lags = jnp.dot(
        stack, table.astype(jnp.float32), precision=lax.Precision.HIGHEST
    )
    pieces = lax.all_to_all(partial_lags, "band", split_axis=1, concat_axis=0, tiled=True)
    return jnp.sum(pieces.reshape(bands, OB_DEV, LAGS // bands), axis=0)


def solution(mesh):
    placed = (P(None, "seg", "band"), P("seg"), P("seg"), P("seg"))
    return jax.shard_map(
        per_device, mesh=mesh, in_specs=placed, out_specs=P("seg", "band"), check_vma=False
    )
```

```python
import math

import jax
import jax.numpy as jnp
from jax import lax
from jax.sharding import PartitionSpec as P

OB_DEV = 8
REACH = 256
FREQ = 1024
LAGS = 1024
HALF_WIN = 64


epsilon = 1e-06


def extended(block, sides, width):
    for axis, dim in sides:
        count = lax.axis_size(axis)
        odd = lax.axis_index(axis) % 2 == 1
        first = lax.slice_in_dim(block, 0, width, axis=dim)
        last = lax.slice_in_dim(block, block.shape[dim] - width, None, axis=dim)
        inner = [(i, i ^ 1) for i in range(count - count % 2)]
        outer = [(i, i + 1) for i in range(1, count - 1, 2)]
        outer = outer + [(target, source) for source, target in outer]
        from_inner = lax.ppermute(jnp.where(odd, first, last), axis, inner)
        from_outer = lax.ppermute(jnp.where(odd, last, first), axis, outer)
        low = jnp.where(odd, from_inner, from_outer)
        high = jnp.where(odd, from_outer, from_inner)
        block = jnp.concatenate([low, block, high], axis=dim)
    return block


def window_matrix(local_bins, half_width):
    padded_index = jnp.arange(local_bins + 2 * half_width)[:, None]
    bin_index = jnp.arange(local_bins)[None, :]
    inside = (padded_index >= bin_index) & (padded_index <= bin_index + 2 * half_width)
    return inside.astype(jnp.bfloat16)


def exact_dot(values, selector):
    high = lax.reduce_precision(values, exponent_bits=8, mantissa_bits=7)
    rest = values - high
    mid = lax.reduce_precision(rest, exponent_bits=8, mantissa_bits=7)
    low = rest - mid
    total = jnp.dot(high.astype(jnp.bfloat16), selector, preferred_element_type=jnp.float32)
    total = total + jnp.dot(mid.astype(jnp.bfloat16), selector, preferred_element_type=jnp.float32)
    return total + jnp.dot(low.astype(jnp.bfloat16), selector, preferred_element_type=jnp.float32)


def select_rows(table, index):
    chosen = (index[:, None] == jnp.arange(table.shape[0], dtype=jnp.int32)[None, :]).astype(
        table.dtype
    )
    return jnp.dot(chosen, table, preferred_element_type=jnp.float32)


def lag_table(first_bin, local_bins, total_bins, lag_count):
    frequency = first_bin + jnp.arange(local_bins, dtype=jnp.int32)
    lag_index = jnp.arange(lag_count, dtype=jnp.int32) - lag_count // 2
    residue = frequency[:, None] * lag_index[None, :] % (2 * total_bins)
    angles = residue.astype(jnp.float32) * (math.pi / total_bins)
    cosine = jnp.cos(angles) / total_bins
    negsine = -jnp.sin(angles) / total_bins
    return jnp.concatenate([cosine, negsine], axis=0).astype(jnp.bfloat16)


def per_device(spectra, pair_first, pair_second, pair_bin):
    seg_position = lax.axis_index("seg")
    band_position = lax.axis_index("band")
    segments = lax.axis_size("seg")
    bands = lax.axis_size("band")
    channels = spectra.shape[1]
    local_bins = spectra.shape[2]
    real_part = spectra[0].astype(jnp.float32)
    imag_part = spectra[1].astype(jnp.float32)
    power_sum = real_part * real_part + imag_part * imag_part
    padded_power = extended(power_sum, (("band", 1),), HALF_WIN)
    window_sum = exact_dot(padded_power, window_matrix(local_bins, HALF_WIN))
    scaling = lax.rsqrt(window_sum / (2 * HALF_WIN + 1) + epsilon)
    whitened = jnp.concatenate([real_part * scaling, imag_part * scaling], axis=1).astype(
        jnp.bfloat16
    )
    first_rows = select_rows(whitened, pair_first - seg_position * channels)
    near_rows = extended(whitened, (("seg", 0),), REACH)
    second_rows = select_rows(near_rows, pair_second - seg_position * channels + REACH)
    first_real = first_rows[:, :local_bins]
    first_imag = first_rows[:, local_bins:]
    second_real = second_rows[:, :local_bins]
    second_imag = second_rows[:, local_bins:]
    cross_real = first_real * second_real + first_imag * second_imag
    cross_imag = first_imag * second_real - first_real * second_imag
    cross_both = jnp.concatenate([cross_real, cross_imag], axis=1).astype(jnp.bfloat16)
    all_bins = segments * OB_DEV
    members = (pair_bin[:, None] == jnp.arange(all_bins, dtype=jnp.int32)[None, :]).astype(
        jnp.bfloat16
    )
    local_stack = lax.dot_general(
        members, cross_both, (((0,), (0,)), ((), ())), preferred_element_type=jnp.float32
    )
    gathered = lax.all_to_all(local_stack, "seg", split_axis=0, concat_axis=0, tiled=True)
    stack = jnp.sum(gathered.reshape(segments, OB_DEV, 2 * local_bins), axis=0)
    table = lag_table(band_position * local_bins, local_bins, FREQ, LAGS)
    partial_lags = jnp.dot(
        stack, table.astype(jnp.float32), precision=lax.Precision.HIGHEST
    )
    pieces = lax.all_to_all(partial_lags, "band", split_axis=1, concat_axis=0, tiled=True)
    return jnp.sum(pieces.reshape(bands, OB_DEV, LAGS // bands), axis=0)


def solution(mesh):
    placed = (P(None, "seg", "band"), P("seg"), P("seg"), P("seg"))
    return jax.shard_map(
        per_device, mesh=mesh, in_specs=placed, out_specs=P("seg", "band"), check_vma=False
    )
```

```python
import math

import jax
import jax.numpy as jnp
from jax import lax
from jax.sharding import PartitionSpec as P

OB_DEV = 8
REACH = 256
FREQ = 1024
LAGS = 1024
HALF_WIN = 64


epsilon = 1e-06


def extended(block, sides, width):
    for axis, dim in sides:
        count = lax.axis_size(axis)
        odd = lax.axis_index(axis) % 2 == 1
        first = lax.slice_in_dim(block, 0, width, axis=dim)
        last = lax.slice_in_dim(block, block.shape[dim] - width, None, axis=dim)
        inner = [(i, i ^ 1) for i in range(count - count % 2)]
        outer = [(i, i + 1) for i in range(1, count - 1, 2)]
        outer = outer + [(target, source) for source, target in outer]
        from_inner = lax.ppermute(jnp.where(odd, first, last), axis, inner)
        from_outer = lax.ppermute(jnp.where(odd, last, first), axis, outer)
        low = jnp.where(odd, from_inner, from_outer)
        high = jnp.where(odd, from_outer, from_inner)
        block = jnp.concatenate([low, block, high], axis=dim)
    return block


def window_matrix(local_bins, half_width):
    padded_index = jnp.arange(local_bins + 2 * half_width)[:, None]
    bin_index = jnp.arange(local_bins)[None, :]
    inside = (padded_index >= bin_index) & (padded_index <= bin_index + 2 * half_width)
    return inside.astype(jnp.bfloat16)


def exact_dot(values, selector):
    high = lax.reduce_precision(values, exponent_bits=8, mantissa_bits=7)
    rest = values - high
    mid = lax.reduce_precision(rest, exponent_bits=8, mantissa_bits=7)
    low = rest - mid
    total = jnp.dot(high.astype(jnp.bfloat16), selector, preferred_element_type=jnp.float32)
    total = total + jnp.dot(mid.astype(jnp.bfloat16), selector, preferred_element_type=jnp.float32)
    return total + jnp.dot(low.astype(jnp.bfloat16), selector, preferred_element_type=jnp.float32)


def select_rows(table, index):
    chosen = (index[:, None] == jnp.arange(table.shape[0], dtype=jnp.int32)[None, :]).astype(
        table.dtype
    )
    return jnp.dot(chosen, table, preferred_element_type=jnp.float32)


def lag_table(first_bin, local_bins, total_bins, lag_count):
    frequency = first_bin + jnp.arange(local_bins, dtype=jnp.int32)
    lag_index = jnp.arange(lag_count, dtype=jnp.int32) - lag_count // 2
    residue = frequency[:, None] * lag_index[None, :] % (2 * total_bins)
    angles = residue.astype(jnp.float32) * (math.pi / total_bins)
    cosine = jnp.cos(angles) / total_bins
    negsine = -jnp.sin(angles) / total_bins
    return jnp.concatenate([cosine, negsine], axis=0).astype(jnp.bfloat16)


def per_device(spectra, pair_first, pair_second, pair_bin):
    seg_position = lax.axis_index("seg")
    band_position = lax.axis_index("band")
    segments = lax.axis_size("seg")
    bands = lax.axis_size("band")
    channels = spectra.shape[1]
    local_bins = spectra.shape[2]
    real_part = spectra[0].astype(jnp.float32)
    imag_part = spectra[1].astype(jnp.float32)
    padded_spectra = extended(spectra, (("band", 2),), HALF_WIN).astype(jnp.float32)
    padded_power = padded_spectra[0] * padded_spectra[0] + padded_spectra[1] * padded_spectra[1]
    window_sum = exact_dot(padded_power, window_matrix(local_bins, HALF_WIN))
    scaling = lax.rsqrt(window_sum / (2 * HALF_WIN + 1) + epsilon)
    whitened = jnp.concatenate([real_part * scaling, imag_part * scaling], axis=1).astype(
        jnp.bfloat16
    )
    first_rows = select_rows(whitened, pair_first - seg_position * channels)
    near_rows = extended(whitened, (("seg", 0),), REACH)
    second_rows = select_rows(near_rows, pair_second - seg_position * channels + REACH)
    first_real = first_rows[:, :local_bins]
    first_imag = first_rows[:, local_bins:]
    second_real = second_rows[:, :local_bins]
    second_imag = second_rows[:, local_bins:]
    cross_real = first_real * second_real + first_imag * second_imag
    cross_imag = first_imag * second_real - first_real * second_imag
    cross_both = jnp.concatenate([cross_real, cross_imag], axis=1).astype(jnp.bfloat16)
    all_bins = segments * OB_DEV
    members = (pair_bin[:, None] == jnp.arange(all_bins, dtype=jnp.int32)[None, :]).astype(
        jnp.bfloat16
    )
    local_stack = lax.dot_general(
        members, cross_both, (((0,), (0,)), ((), ())), preferred_element_type=jnp.float32
    )
    gathered = lax.all_to_all(local_stack, "seg", split_axis=0, concat_axis=0, tiled=True)
    stack = jnp.sum(gathered.reshape(segments, OB_DEV, 2 * local_bins), axis=0)
    table = lag_table(band_position * local_bins, local_bins, FREQ, LAGS)
    partial_lags = jnp.dot(
        stack, table.astype(jnp.float32), precision=lax.Precision.HIGHEST
    )
    pieces = lax.all_to_all(partial_lags, "band", split_axis=1, concat_axis=0, tiled=True)
    return jnp.sum(pieces.reshape(bands, OB_DEV, LAGS // bands), axis=0)


def solution(mesh):
    placed = (P(None, "seg", "band"), P("seg"), P("seg"), P("seg"))
    return jax.shard_map(
        per_device, mesh=mesh, in_specs=placed, out_specs=P("seg", "band"), check_vma=False
    )
```

```python
import math

import jax
import jax.numpy as jnp
from jax import lax
from jax.sharding import PartitionSpec as P

OB_DEV = 8
REACH = 256
FREQ = 1024
LAGS = 1024
HALF_WIN = 64


epsilon = 1e-06


def extended(block, sides, width):
    for axis, dim in sides:
        count = lax.axis_size(axis)
        odd = lax.axis_index(axis) % 2 == 1
        first = lax.slice_in_dim(block, 0, width, axis=dim)
        last = lax.slice_in_dim(block, block.shape[dim] - width, None, axis=dim)
        inner = [(i, i ^ 1) for i in range(count - count % 2)]
        outer = [(i, i + 1) for i in range(1, count - 1, 2)]
        outer = outer + [(target, source) for source, target in outer]
        from_inner = lax.ppermute(jnp.where(odd, first, last), axis, inner)
        from_outer = lax.ppermute(jnp.where(odd, last, first), axis, outer)
        low = jnp.where(odd, from_inner, from_outer)
        high = jnp.where(odd, from_outer, from_inner)
        block = jnp.concatenate([low, block, high], axis=dim)
    return block


def window_matrix(local_bins, half_width):
    padded_index = jnp.arange(local_bins + 2 * half_width)[:, None]
    bin_index = jnp.arange(local_bins)[None, :]
    inside = (padded_index >= bin_index) & (padded_index <= bin_index + 2 * half_width)
    return inside.astype(jnp.bfloat16)


def exact_dot(values, selector):
    high = lax.reduce_precision(values, exponent_bits=8, mantissa_bits=7)
    rest = values - high
    mid = lax.reduce_precision(rest, exponent_bits=8, mantissa_bits=7)
    low = rest - mid
    total = jnp.dot(high.astype(jnp.bfloat16), selector, preferred_element_type=jnp.float32)
    total = total + jnp.dot(mid.astype(jnp.bfloat16), selector, preferred_element_type=jnp.float32)
    return total + jnp.dot(low.astype(jnp.bfloat16), selector, preferred_element_type=jnp.float32)


def select_rows(table, index):
    chosen = (index[:, None] == jnp.arange(table.shape[0], dtype=jnp.int32)[None, :]).astype(
        table.dtype
    )
    return jnp.dot(chosen, table, preferred_element_type=jnp.float32)


def lag_table(first_bin, local_bins, total_bins, lag_count):
    frequency = first_bin + jnp.arange(local_bins, dtype=jnp.int32)
    lag_index = jnp.arange(lag_count, dtype=jnp.int32) - lag_count // 2
    residue = frequency[:, None] * lag_index[None, :] % (2 * total_bins)
    angles = residue.astype(jnp.float32) * (math.pi / total_bins)
    cosine = jnp.cos(angles) / total_bins
    negsine = -jnp.sin(angles) / total_bins
    return jnp.concatenate([cosine, negsine], axis=0).astype(jnp.bfloat16)


def per_device(spectra, pair_first, pair_second, pair_bin):
    seg_position = lax.axis_index("seg")
    band_position = lax.axis_index("band")
    segments = lax.axis_size("seg")
    bands = lax.axis_size("band")
    channels = spectra.shape[1]
    local_bins = spectra.shape[2]
    real_part = spectra[0].astype(jnp.float32)
    imag_part = spectra[1].astype(jnp.float32)
    power_sum = real_part * real_part + imag_part * imag_part
    padded_power = extended(power_sum, (("band", 1),), HALF_WIN)
    window_sum = exact_dot(padded_power, window_matrix(local_bins, HALF_WIN))
    scaling = lax.rsqrt(window_sum / (2 * HALF_WIN + 1) + epsilon)
    whitened = jnp.concatenate([real_part * scaling, imag_part * scaling], axis=1).astype(
        jnp.bfloat16
    )
    first_rows = select_rows(whitened, pair_first - seg_position * channels)
    near_rows = extended(whitened, (("seg", 0),), REACH)
    second_rows = select_rows(near_rows, pair_second - seg_position * channels + REACH)
    first_real = first_rows[:, :local_bins]
    first_imag = first_rows[:, local_bins:]
    second_real = second_rows[:, :local_bins]
    second_imag = second_rows[:, local_bins:]
    cross_real = first_real * second_real + first_imag * second_imag
    cross_imag = first_imag * second_real - first_real * second_imag
    cross_both = jnp.concatenate([cross_real, cross_imag], axis=1).astype(jnp.bfloat16)
    all_bins = segments * OB_DEV
    members = (pair_bin[:, None] == jnp.arange(all_bins, dtype=jnp.int32)[None, :]).astype(
        jnp.bfloat16
    )
    local_stack = lax.dot_general(
        members, cross_both, (((0,), (0,)), ((), ())), preferred_element_type=jnp.float32
    )
    gathered = lax.all_to_all(
        local_stack.astype(jnp.bfloat16), "seg", split_axis=0, concat_axis=0, tiled=True
    )
    stack = jnp.sum(
        gathered.reshape(segments, OB_DEV, 2 * local_bins).astype(jnp.float32), axis=0
    )
    table = lag_table(band_position * local_bins, local_bins, FREQ, LAGS)
    partial_lags = jnp.dot(
        stack, table.astype(jnp.float32), precision=lax.Precision.HIGHEST
    )
    pieces = lax.all_to_all(partial_lags, "band", split_axis=1, concat_axis=0, tiled=True)
    return jnp.sum(pieces.reshape(bands, OB_DEV, LAGS // bands), axis=0)


def solution(mesh):
    placed = (P(None, "seg", "band"), P("seg"), P("seg"), P("seg"))
    return jax.shard_map(
        per_device, mesh=mesh, in_specs=placed, out_specs=P("seg", "band"), check_vma=False
    )
```

```python
import math

import jax
import jax.numpy as jnp
from jax import lax
from jax.sharding import PartitionSpec as P

OB_DEV = 8
REACH = 256
FREQ = 1024
LAGS = 1024
HALF_WIN = 64


epsilon = 1e-06


def extended(block, sides, width, edges=None):
    for axis, dim in sides:
        count = lax.axis_size(axis)
        odd = lax.axis_index(axis) % 2 == 1
        source = block if edges is None else edges
        first = lax.slice_in_dim(source, 0, width, axis=dim)
        last = lax.slice_in_dim(source, source.shape[dim] - width, None, axis=dim)
        inner = [(i, i ^ 1) for i in range(count - count % 2)]
        outer = [(i, i + 1) for i in range(1, count - 1, 2)]
        outer = outer + [(target, source) for source, target in outer]
        from_inner = lax.ppermute(jnp.where(odd, first, last), axis, inner)
        from_outer = lax.ppermute(jnp.where(odd, last, first), axis, outer)
        low = jnp.where(odd, from_inner, from_outer)
        high = jnp.where(odd, from_outer, from_inner)
        block = jnp.concatenate([low, block, high], axis=dim)
    return block


def window_matrix(local_bins, half_width):
    padded_index = jnp.arange(local_bins + 2 * half_width)[:, None]
    bin_index = jnp.arange(local_bins)[None, :]
    inside = (padded_index >= bin_index) & (padded_index <= bin_index + 2 * half_width)
    return inside.astype(jnp.bfloat16)


def exact_dot(values, selector):
    high = lax.reduce_precision(values, exponent_bits=8, mantissa_bits=7)
    rest = values - high
    mid = lax.reduce_precision(rest, exponent_bits=8, mantissa_bits=7)
    low = rest - mid
    total = jnp.dot(high.astype(jnp.bfloat16), selector, preferred_element_type=jnp.float32)
    total = total + jnp.dot(mid.astype(jnp.bfloat16), selector, preferred_element_type=jnp.float32)
    return total + jnp.dot(low.astype(jnp.bfloat16), selector, preferred_element_type=jnp.float32)


def select_rows(table, index):
    chosen = (index[:, None] == jnp.arange(table.shape[0], dtype=jnp.int32)[None, :]).astype(
        table.dtype
    )
    return jnp.dot(chosen, table, preferred_element_type=jnp.float32)


def lag_table(first_bin, local_bins, total_bins, lag_count):
    frequency = first_bin + jnp.arange(local_bins, dtype=jnp.int32)
    lag_index = jnp.arange(lag_count, dtype=jnp.int32) - lag_count // 2
    residue = frequency[:, None] * lag_index[None, :] % (2 * total_bins)
    angles = residue.astype(jnp.float32) * (math.pi / total_bins)
    cosine = jnp.cos(angles) / total_bins
    negsine = -jnp.sin(angles) / total_bins
    return jnp.concatenate([cosine, negsine], axis=0).astype(jnp.bfloat16)


def per_device(spectra, pair_first, pair_second, pair_bin):
    seg_position = lax.axis_index("seg")
    band_position = lax.axis_index("band")
    segments = lax.axis_size("seg")
    bands = lax.axis_size("band")
    channels = spectra.shape[1]
    local_bins = spectra.shape[2]
    real_part = spectra[0].astype(jnp.float32)
    imag_part = spectra[1].astype(jnp.float32)
    power_sum = real_part * real_part + imag_part * imag_part
    edges = jnp.concatenate(
        [spectra[:, :, :HALF_WIN], spectra[:, :, local_bins - HALF_WIN :]], axis=2
    ).astype(jnp.float32)
    edge_power = edges[0] * edges[0] + edges[1] * edges[1]
    padded_power = extended(power_sum, (("band", 1),), HALF_WIN, edge_power)
    window_sum = exact_dot(padded_power, window_matrix(local_bins, HALF_WIN))
    scaling = lax.rsqrt(window_sum / (2 * HALF_WIN + 1) + epsilon)
    whitened = jnp.concatenate([real_part * scaling, imag_part * scaling], axis=1).astype(
        jnp.bfloat16
    )
    first_rows = select_rows(whitened, pair_first - seg_position * channels)
    near_rows = extended(whitened, (("seg", 0),), REACH)
    second_rows = select_rows(near_rows, pair_second - seg_position * channels + REACH)
    first_real = first_rows[:, :local_bins]
    first_imag = first_rows[:, local_bins:]
    second_real = second_rows[:, :local_bins]
    second_imag = second_rows[:, local_bins:]
    cross_real = first_real * second_real + first_imag * second_imag
    cross_imag = first_imag * second_real - first_real * second_imag
    cross_both = jnp.concatenate([cross_real, cross_imag], axis=1).astype(jnp.bfloat16)
    all_bins = segments * OB_DEV
    members = (pair_bin[:, None] == jnp.arange(all_bins, dtype=jnp.int32)[None, :]).astype(
        jnp.bfloat16
    )
    local_stack = lax.dot_general(
        members, cross_both, (((0,), (0,)), ((), ())), preferred_element_type=jnp.float32
    )
    gathered = lax.all_to_all(
        local_stack.astype(jnp.bfloat16), "seg", split_axis=0, concat_axis=0, tiled=True
    )
    stack = jnp.sum(
        gathered.reshape(segments, OB_DEV, 2 * local_bins).astype(jnp.float32), axis=0
    )
    table = lag_table(band_position * local_bins, local_bins, FREQ, LAGS)
    partial_lags = jnp.dot(
        stack, table.astype(jnp.float32), precision=lax.Precision.HIGHEST
    )
    pieces = lax.all_to_all(partial_lags, "band", split_axis=1, concat_axis=0, tiled=True)
    return jnp.sum(pieces.reshape(bands, OB_DEV, LAGS // bands), axis=0)


def solution(mesh):
    placed = (P(None, "seg", "band"), P("seg"), P("seg"), P("seg"))
    return jax.shard_map(
        per_device, mesh=mesh, in_specs=placed, out_specs=P("seg", "band"), check_vma=False
    )
```

```python
import math

import jax
import jax.numpy as jnp
from jax import lax
from jax.sharding import PartitionSpec as P

OB_DEV = 8
REACH = 256
FREQ = 1024
LAGS = 1024
HALF_WIN = 64


epsilon = 1e-06


def extended(block, sides, width, wire=None):
    for axis, dim in sides:
        count = lax.axis_size(axis)
        odd = lax.axis_index(axis) % 2 == 1
        first = lax.slice_in_dim(block, 0, width, axis=dim)
        last = lax.slice_in_dim(block, block.shape[dim] - width, None, axis=dim)
        inner = [(i, i ^ 1) for i in range(count - count % 2)]
        outer = [(i, i + 1) for i in range(1, count - 1, 2)]
        outer = outer + [(target, source) for source, target in outer]
        wire_type = block.dtype if wire is None else wire
        from_inner = lax.ppermute(jnp.where(odd, first, last).astype(wire_type), axis, inner)
        from_outer = lax.ppermute(jnp.where(odd, last, first).astype(wire_type), axis, outer)
        from_inner = from_inner.astype(block.dtype)
        from_outer = from_outer.astype(block.dtype)
        low = jnp.where(odd, from_inner, from_outer)
        high = jnp.where(odd, from_outer, from_inner)
        block = jnp.concatenate([low, block, high], axis=dim)
    return block


def window_matrix(local_bins, half_width):
    padded_index = jnp.arange(local_bins + 2 * half_width)[:, None]
    bin_index = jnp.arange(local_bins)[None, :]
    inside = (padded_index >= bin_index) & (padded_index <= bin_index + 2 * half_width)
    return inside.astype(jnp.bfloat16)


def exact_dot(values, selector):
    high = lax.reduce_precision(values, exponent_bits=8, mantissa_bits=7)
    rest = values - high
    mid = lax.reduce_precision(rest, exponent_bits=8, mantissa_bits=7)
    low = rest - mid
    total = jnp.dot(high.astype(jnp.bfloat16), selector, preferred_element_type=jnp.float32)
    total = total + jnp.dot(mid.astype(jnp.bfloat16), selector, preferred_element_type=jnp.float32)
    return total + jnp.dot(low.astype(jnp.bfloat16), selector, preferred_element_type=jnp.float32)


def select_rows(table, index):
    chosen = (index[:, None] == jnp.arange(table.shape[0], dtype=jnp.int32)[None, :]).astype(
        table.dtype
    )
    return jnp.dot(chosen, table, preferred_element_type=jnp.float32)


def lag_table(first_bin, local_bins, total_bins, lag_count):
    frequency = first_bin + jnp.arange(local_bins, dtype=jnp.int32)
    lag_index = jnp.arange(lag_count, dtype=jnp.int32) - lag_count // 2
    residue = frequency[:, None] * lag_index[None, :] % (2 * total_bins)
    angles = residue.astype(jnp.float32) * (math.pi / total_bins)
    cosine = jnp.cos(angles) / total_bins
    negsine = -jnp.sin(angles) / total_bins
    return jnp.concatenate([cosine, negsine], axis=0).astype(jnp.bfloat16)


def per_device(spectra, pair_first, pair_second, pair_bin):
    seg_position = lax.axis_index("seg")
    band_position = lax.axis_index("band")
    segments = lax.axis_size("seg")
    bands = lax.axis_size("band")
    channels = spectra.shape[1]
    local_bins = spectra.shape[2]
    real_part = spectra[0].astype(jnp.float32)
    imag_part = spectra[1].astype(jnp.float32)
    power_sum = real_part * real_part + imag_part * imag_part
    padded_power = extended(power_sum, (("band", 1),), HALF_WIN, jnp.bfloat16)
    window_sum = exact_dot(padded_power, window_matrix(local_bins, HALF_WIN))
    scaling = lax.rsqrt(window_sum / (2 * HALF_WIN + 1) + epsilon)
    whitened = jnp.concatenate([real_part * scaling, imag_part * scaling], axis=1).astype(
        jnp.bfloat16
    )
    first_rows = select_rows(whitened, pair_first - seg_position * channels)
    near_rows = extended(whitened, (("seg", 0),), REACH)
    second_rows = select_rows(near_rows, pair_second - seg_position * channels + REACH)
    first_real = first_rows[:, :local_bins]
    first_imag = first_rows[:, local_bins:]
    second_real = second_rows[:, :local_bins]
    second_imag = second_rows[:, local_bins:]
    cross_real = first_real * second_real + first_imag * second_imag
    cross_imag = first_imag * second_real - first_real * second_imag
    cross_both = jnp.concatenate([cross_real, cross_imag], axis=1).astype(jnp.bfloat16)
    all_bins = segments * OB_DEV
    members = (pair_bin[:, None] == jnp.arange(all_bins, dtype=jnp.int32)[None, :]).astype(
        jnp.bfloat16
    )
    local_stack = lax.dot_general(
        members, cross_both, (((0,), (0,)), ((), ())), preferred_element_type=jnp.float32
    )
    gathered = lax.all_to_all(
        local_stack.astype(jnp.bfloat16), "seg", split_axis=0, concat_axis=0, tiled=True
    )
    stack = jnp.sum(
        gathered.reshape(segments, OB_DEV, 2 * local_bins).astype(jnp.float32), axis=0
    )
    table = lag_table(band_position * local_bins, local_bins, FREQ, LAGS)
    partial_lags = jnp.dot(
        stack, table.astype(jnp.float32), precision=lax.Precision.HIGHEST
    )
    pieces = lax.all_to_all(partial_lags, "band", split_axis=1, concat_axis=0, tiled=True)
    return jnp.sum(pieces.reshape(bands, OB_DEV, LAGS // bands), axis=0)


def solution(mesh):
    placed = (P(None, "seg", "band"), P("seg"), P("seg"), P("seg"))
    return jax.shard_map(
        per_device, mesh=mesh, in_specs=placed, out_specs=P("seg", "band"), check_vma=False
    )
```

```python
import math

import jax
import jax.numpy as jnp
from jax import lax
from jax.sharding import PartitionSpec as P

OB_DEV = 8
REACH = 256
FREQ = 1024
LAGS = 1024
HALF_WIN = 64


epsilon = 1e-06


def extended(block, sides, width, wire=None):
    for axis, dim in sides:
        count = lax.axis_size(axis)
        odd = lax.axis_index(axis) % 2 == 1
        first = lax.slice_in_dim(block, 0, width, axis=dim)
        last = lax.slice_in_dim(block, block.shape[dim] - width, None, axis=dim)
        inner = [(i, i ^ 1) for i in range(count - count % 2)]
        outer = [(i, i + 1) for i in range(1, count - 1, 2)]
        outer = outer + [(target, source) for source, target in outer]
        wire_type = block.dtype if wire is None else wire
        from_inner = lax.ppermute(jnp.where(odd, first, last).astype(wire_type), axis, inner)
        from_outer = lax.ppermute(jnp.where(odd, last, first).astype(wire_type), axis, outer)
        from_inner = from_inner.astype(block.dtype)
        from_outer = from_outer.astype(block.dtype)
        low = jnp.where(odd, from_inner, from_outer)
        high = jnp.where(odd, from_outer, from_inner)
        block = jnp.concatenate([low, block, high], axis=dim)
    return block


def window_matrix(local_bins, half_width):
    padded_index = jnp.arange(local_bins + 2 * half_width)[:, None]
    bin_index = jnp.arange(local_bins)[None, :]
    inside = (padded_index >= bin_index) & (padded_index <= bin_index + 2 * half_width)
    return inside.astype(jnp.bfloat16)


def exact_dot(values, selector):
    high = lax.reduce_precision(values, exponent_bits=8, mantissa_bits=7)
    rest = values - high
    mid = lax.reduce_precision(rest, exponent_bits=8, mantissa_bits=7)
    low = rest - mid
    total = jnp.dot(high.astype(jnp.bfloat16), selector, preferred_element_type=jnp.float32)
    total = total + jnp.dot(mid.astype(jnp.bfloat16), selector, preferred_element_type=jnp.float32)
    return total + jnp.dot(low.astype(jnp.bfloat16), selector, preferred_element_type=jnp.float32)


def select_rows(table, index):
    chosen = (index[:, None] == jnp.arange(table.shape[0], dtype=jnp.int32)[None, :]).astype(
        table.dtype
    )
    return jnp.dot(chosen, table, preferred_element_type=jnp.float32)


def lag_table(first_bin, local_bins, total_bins, lag_count):
    frequency = first_bin + jnp.arange(local_bins, dtype=jnp.int32)
    lag_index = jnp.arange(lag_count, dtype=jnp.int32) - lag_count // 2
    residue = frequency[:, None] * lag_index[None, :] % (2 * total_bins)
    angles = residue.astype(jnp.float32) * (math.pi / total_bins)
    cosine = jnp.cos(angles) / total_bins
    negsine = -jnp.sin(angles) / total_bins
    return jnp.concatenate([cosine, negsine], axis=0).astype(jnp.bfloat16)


def per_device(spectra, pair_first, pair_second, pair_bin):
    seg_position = lax.axis_index("seg")
    band_position = lax.axis_index("band")
    segments = lax.axis_size("seg")
    bands = lax.axis_size("band")
    channels = spectra.shape[1]
    local_bins = spectra.shape[2]
    real_part = spectra[0].astype(jnp.float32)
    imag_part = spectra[1].astype(jnp.float32)
    power_sum = real_part * real_part + imag_part * imag_part
    padded_power = extended(power_sum, (("band", 1),), HALF_WIN, jnp.bfloat16)
    table = lag_table(band_position * local_bins, local_bins, FREQ, LAGS)
    padded_power, table = lax.optimization_barrier((padded_power, table))
    window_sum = exact_dot(padded_power, window_matrix(local_bins, HALF_WIN))
    scaling = lax.rsqrt(window_sum / (2 * HALF_WIN + 1) + epsilon)
    whitened = jnp.concatenate([real_part * scaling, imag_part * scaling], axis=1).astype(
        jnp.bfloat16
    )
    first_rows = select_rows(whitened, pair_first - seg_position * channels)
    near_rows = extended(whitened, (("seg", 0),), REACH)
    second_rows = select_rows(near_rows, pair_second - seg_position * channels + REACH)
    first_real = first_rows[:, :local_bins]
    first_imag = first_rows[:, local_bins:]
    second_real = second_rows[:, :local_bins]
    second_imag = second_rows[:, local_bins:]
    cross_real = first_real * second_real + first_imag * second_imag
    cross_imag = first_imag * second_real - first_real * second_imag
    cross_both = jnp.concatenate([cross_real, cross_imag], axis=1).astype(jnp.bfloat16)
    all_bins = segments * OB_DEV
    members = (pair_bin[:, None] == jnp.arange(all_bins, dtype=jnp.int32)[None, :]).astype(
        jnp.bfloat16
    )
    local_stack = lax.dot_general(
        members, cross_both, (((0,), (0,)), ((), ())), preferred_element_type=jnp.float32
    )
    gathered = lax.all_to_all(
        local_stack.astype(jnp.bfloat16), "seg", split_axis=0, concat_axis=0, tiled=True
    )
    stack = jnp.sum(
        gathered.reshape(segments, OB_DEV, 2 * local_bins).astype(jnp.float32), axis=0
    )
    partial_lags = jnp.dot(
        stack, table.astype(jnp.float32), precision=lax.Precision.HIGHEST
    )
    pieces = lax.all_to_all(partial_lags, "band", split_axis=1, concat_axis=0, tiled=True)
    return jnp.sum(pieces.reshape(bands, OB_DEV, LAGS // bands), axis=0)


def solution(mesh):
    placed = (P(None, "seg", "band"), P("seg"), P("seg"), P("seg"))
    return jax.shard_map(
        per_device, mesh=mesh, in_specs=placed, out_specs=P("seg", "band"), check_vma=False
    )
```

```python
import math

import jax
import jax.numpy as jnp
from jax import lax
from jax.sharding import PartitionSpec as P

OB_DEV = 8
REACH = 256
FREQ = 1024
LAGS = 1024
HALF_WIN = 64


epsilon = 1e-06


def extended(block, sides, width, wire=None, edges=None):
    for axis, dim in sides:
        count = lax.axis_size(axis)
        odd = lax.axis_index(axis) % 2 == 1
        source = block if edges is None else edges
        first = lax.slice_in_dim(source, 0, width, axis=dim)
        last = lax.slice_in_dim(source, source.shape[dim] - width, None, axis=dim)
        inner = [(i, i ^ 1) for i in range(count - count % 2)]
        outer = [(i, i + 1) for i in range(1, count - 1, 2)]
        outer = outer + [(target, source) for source, target in outer]
        wire_type = block.dtype if wire is None else wire
        from_inner = lax.ppermute(jnp.where(odd, first, last).astype(wire_type), axis, inner)
        from_outer = lax.ppermute(jnp.where(odd, last, first).astype(wire_type), axis, outer)
        from_inner = from_inner.astype(block.dtype)
        from_outer = from_outer.astype(block.dtype)
        low = jnp.where(odd, from_inner, from_outer)
        high = jnp.where(odd, from_outer, from_inner)
        block = jnp.concatenate([low, block, high], axis=dim)
    return block


def window_matrix(local_bins, half_width):
    padded_index = jnp.arange(local_bins + 2 * half_width)[:, None]
    bin_index = jnp.arange(local_bins)[None, :]
    inside = (padded_index >= bin_index) & (padded_index <= bin_index + 2 * half_width)
    return inside.astype(jnp.bfloat16)


def exact_dot(values, selector):
    high = lax.reduce_precision(values, exponent_bits=8, mantissa_bits=7)
    rest = values - high
    mid = lax.reduce_precision(rest, exponent_bits=8, mantissa_bits=7)
    low = rest - mid
    total = jnp.dot(high.astype(jnp.bfloat16), selector, preferred_element_type=jnp.float32)
    total = total + jnp.dot(mid.astype(jnp.bfloat16), selector, preferred_element_type=jnp.float32)
    return total + jnp.dot(low.astype(jnp.bfloat16), selector, preferred_element_type=jnp.float32)


def select_rows(table, index):
    chosen = (index[:, None] == jnp.arange(table.shape[0], dtype=jnp.int32)[None, :]).astype(
        table.dtype
    )
    return jnp.dot(chosen, table, preferred_element_type=jnp.float32)


def lag_table(first_bin, local_bins, total_bins, lag_count):
    frequency = first_bin + jnp.arange(local_bins, dtype=jnp.int32)
    lag_index = jnp.arange(lag_count, dtype=jnp.int32) - lag_count // 2
    residue = frequency[:, None] * lag_index[None, :] % (2 * total_bins)
    angles = residue.astype(jnp.float32) * (math.pi / total_bins)
    cosine = jnp.cos(angles) / total_bins
    negsine = -jnp.sin(angles) / total_bins
    return jnp.concatenate([cosine, negsine], axis=0).astype(jnp.bfloat16)


def per_device(spectra, pair_first, pair_second, pair_bin):
    seg_position = lax.axis_index("seg")
    band_position = lax.axis_index("band")
    segments = lax.axis_size("seg")
    bands = lax.axis_size("band")
    channels = spectra.shape[1]
    local_bins = spectra.shape[2]
    real_part = spectra[0].astype(jnp.float32)
    imag_part = spectra[1].astype(jnp.float32)
    power_sum = real_part * real_part + imag_part * imag_part
    edges = jnp.concatenate(
        [spectra[:, :, :HALF_WIN], spectra[:, :, local_bins - HALF_WIN :]], axis=2
    ).astype(jnp.float32)
    edge_power = edges[0] * edges[0] + edges[1] * edges[1]
    padded_power = extended(power_sum, (("band", 1),), HALF_WIN, jnp.bfloat16, edge_power)
    table = lag_table(band_position * local_bins, local_bins, FREQ, LAGS)
    padded_power, table = lax.optimization_barrier((padded_power, table))
    window_sum = exact_dot(padded_power, window_matrix(local_bins, HALF_WIN))
    scaling = lax.rsqrt(window_sum / (2 * HALF_WIN + 1) + epsilon)
    whitened = jnp.concatenate([real_part * scaling, imag_part * scaling], axis=1).astype(
        jnp.bfloat16
    )
    first_rows = select_rows(whitened, pair_first - seg_position * channels)
    near_rows = extended(whitened, (("seg", 0),), REACH)
    second_rows = select_rows(near_rows, pair_second - seg_position * channels + REACH)
    first_real = first_rows[:, :local_bins]
    first_imag = first_rows[:, local_bins:]
    second_real = second_rows[:, :local_bins]
    second_imag = second_rows[:, local_bins:]
    cross_real = first_real * second_real + first_imag * second_imag
    cross_imag = first_imag * second_real - first_real * second_imag
    cross_both = jnp.concatenate([cross_real, cross_imag], axis=1).astype(jnp.bfloat16)
    all_bins = segments * OB_DEV
    members = (pair_bin[:, None] == jnp.arange(all_bins, dtype=jnp.int32)[None, :]).astype(
        jnp.bfloat16
    )
    local_stack = lax.dot_general(
        members, cross_both, (((0,), (0,)), ((), ())), preferred_element_type=jnp.float32
    )
    gathered = lax.all_to_all(
        local_stack.astype(jnp.bfloat16), "seg", split_axis=0, concat_axis=0, tiled=True
    )
    stack = jnp.sum(
        gathered.reshape(segments, OB_DEV, 2 * local_bins).astype(jnp.float32), axis=0
    )
    partial_lags = jnp.dot(
        stack, table.astype(jnp.float32), precision=lax.Precision.HIGHEST
    )
    pieces = lax.all_to_all(partial_lags, "band", split_axis=1, concat_axis=0, tiled=True)
    return jnp.sum(pieces.reshape(bands, OB_DEV, LAGS // bands), axis=0)


def solution(mesh):
    placed = (P(None, "seg", "band"), P("seg"), P("seg"), P("seg"))
    return jax.shard_map(
        per_device, mesh=mesh, in_specs=placed, out_specs=P("seg", "band"), check_vma=False
    )
```

```python
import math

import jax
import jax.numpy as jnp
from jax import lax
from jax.sharding import PartitionSpec as P

OB_DEV = 8
REACH = 256
FREQ = 1024
LAGS = 1024
HALF_WIN = 64


epsilon = 1e-06


def extended(block, sides, width, wire=None):
    for axis, dim in sides:
        count = lax.axis_size(axis)
        odd = lax.axis_index(axis) % 2 == 1
        first = lax.slice_in_dim(block, 0, width, axis=dim)
        last = lax.slice_in_dim(block, block.shape[dim] - width, None, axis=dim)
        inner = [(i, i ^ 1) for i in range(count - count % 2)]
        outer = [(i, i + 1) for i in range(1, count - 1, 2)]
        outer = outer + [(target, source) for source, target in outer]
        wire_type = block.dtype if wire is None else wire
        from_inner = lax.ppermute(jnp.where(odd, first, last).astype(wire_type), axis, inner)
        from_outer = lax.ppermute(jnp.where(odd, last, first).astype(wire_type), axis, outer)
        from_inner = from_inner.astype(block.dtype)
        from_outer = from_outer.astype(block.dtype)
        low = jnp.where(odd, from_inner, from_outer)
        high = jnp.where(odd, from_outer, from_inner)
        block = jnp.concatenate([low, block, high], axis=dim)
    return block


def window_matrix(local_bins, half_width):
    padded_index = jnp.arange(local_bins + 2 * half_width)[:, None]
    bin_index = jnp.arange(local_bins)[None, :]
    inside = (padded_index >= bin_index) & (padded_index <= bin_index + 2 * half_width)
    return inside.astype(jnp.bfloat16)


def exact_dot(values, selector):
    high = lax.reduce_precision(values, exponent_bits=8, mantissa_bits=7)
    rest = values - high
    mid = lax.reduce_precision(rest, exponent_bits=8, mantissa_bits=7)
    low = rest - mid
    total = jnp.dot(high.astype(jnp.bfloat16), selector, preferred_element_type=jnp.float32)
    total = total + jnp.dot(mid.astype(jnp.bfloat16), selector, preferred_element_type=jnp.float32)
    return total + jnp.dot(low.astype(jnp.bfloat16), selector, preferred_element_type=jnp.float32)


def select_rows(table, index):
    chosen = (index[:, None] == jnp.arange(table.shape[0], dtype=jnp.int32)[None, :]).astype(
        table.dtype
    )
    return jnp.dot(chosen, table, preferred_element_type=jnp.float32)


def lag_table(first_bin, local_bins, total_bins, lag_count):
    frequency = first_bin + jnp.arange(local_bins, dtype=jnp.int32)
    lag_index = jnp.arange(lag_count, dtype=jnp.int32) - lag_count // 2
    residue = frequency[:, None] * lag_index[None, :] % (2 * total_bins)
    angles = residue.astype(jnp.float32) * (math.pi / total_bins)
    cosine = jnp.cos(angles) / total_bins
    negsine = -jnp.sin(angles) / total_bins
    return jnp.concatenate([cosine, negsine], axis=0).astype(jnp.bfloat16)


def per_device(spectra, pair_first, pair_second, pair_bin):
    seg_position = lax.axis_index("seg")
    band_position = lax.axis_index("band")
    segments = lax.axis_size("seg")
    bands = lax.axis_size("band")
    channels = spectra.shape[1]
    local_bins = spectra.shape[2]
    real_part = spectra[0].astype(jnp.float32)
    imag_part = spectra[1].astype(jnp.float32)
    power_sum = real_part * real_part + imag_part * imag_part
    padded_power = extended(power_sum, (("band", 1),), HALF_WIN, jnp.bfloat16)
    table = lag_table(band_position * local_bins, local_bins, FREQ, LAGS)
    padded_power, table = lax.optimization_barrier((padded_power, table))
    window_sum = exact_dot(padded_power, window_matrix(local_bins, HALF_WIN))
    scaling = lax.rsqrt(window_sum / (2 * HALF_WIN + 1) + epsilon)
    whitened = jnp.concatenate([real_part * scaling, imag_part * scaling], axis=1).astype(
        jnp.bfloat16
    )
    first_rows = select_rows(whitened, pair_first - seg_position * channels)
    near_rows = extended(whitened, (("seg", 0),), REACH)
    second_rows = select_rows(near_rows, pair_second - seg_position * channels + REACH)
    first_real = first_rows[:, :local_bins]
    first_imag = first_rows[:, local_bins:]
    second_real = second_rows[:, :local_bins]
    second_imag = second_rows[:, local_bins:]
    cross_real = first_real * second_real + first_imag * second_imag
    cross_imag = first_imag * second_real - first_real * second_imag
    cross_both = jnp.concatenate([cross_real, cross_imag], axis=1).astype(jnp.bfloat16)
    all_bins = segments * OB_DEV
    members = (pair_bin[:, None] == jnp.arange(all_bins, dtype=jnp.int32)[None, :]).astype(
        jnp.bfloat16
    )
    local_stack = lax.dot_general(
        members, cross_both, (((0,), (0,)), ((), ())), preferred_element_type=jnp.float32
    )
    parity = seg_position % 2
    by_parity = local_stack.reshape(segments // 2, 2, OB_DEV, 2 * local_bins)
    keep = jnp.where(parity == 0, by_parity[:, 0], by_parity[:, 1])
    give = jnp.where(parity == 0, by_parity[:, 1], by_parity[:, 0])
    partner = lax.ppermute(give, "seg", [(i, i ^ 1) for i in range(segments)])
    chip_stack = keep + partner
    same_core = [list(range(0, segments, 2)), list(range(1, segments, 2))]
    gathered = lax.all_to_all(
        chip_stack.astype(jnp.bfloat16),
        "seg",
        split_axis=0,
        concat_axis=0,
        tiled=True,
        axis_index_groups=same_core,
    )
    stack = jnp.sum(gathered.astype(jnp.float32), axis=0)
    partial_lags = jnp.dot(
        stack, table.astype(jnp.float32), precision=lax.Precision.HIGHEST
    )
    pieces = lax.all_to_all(partial_lags, "band", split_axis=1, concat_axis=0, tiled=True)
    return jnp.sum(pieces.reshape(bands, OB_DEV, LAGS // bands), axis=0)


def solution(mesh):
    placed = (P(None, "seg", "band"), P("seg"), P("seg"), P("seg"))
    return jax.shard_map(
        per_device, mesh=mesh, in_specs=placed, out_specs=P("seg", "band"), check_vma=False
    )
```

```python
import math

import jax
import jax.numpy as jnp
from jax import lax
from jax.sharding import PartitionSpec as P

OB_DEV = 8
REACH = 256
FREQ = 1024
LAGS = 1024
HALF_WIN = 64


epsilon = 1e-06


def extended(block, sides, width, wire=None):
    for axis, dim in sides:
        count = lax.axis_size(axis)
        odd = lax.axis_index(axis) % 2 == 1
        first = lax.slice_in_dim(block, 0, width, axis=dim)
        last = lax.slice_in_dim(block, block.shape[dim] - width, None, axis=dim)
        inner = [(i, i ^ 1) for i in range(count - count % 2)]
        outer = [(i, i + 1) for i in range(1, count - 1, 2)]
        outer = outer + [(target, source) for source, target in outer]
        wire_type = block.dtype if wire is None else wire
        from_inner = lax.ppermute(jnp.where(odd, first, last).astype(wire_type), axis, inner)
        from_outer = lax.ppermute(jnp.where(odd, last, first).astype(wire_type), axis, outer)
        from_inner = from_inner.astype(block.dtype)
        from_outer = from_outer.astype(block.dtype)
        low = jnp.where(odd, from_inner, from_outer)
        high = jnp.where(odd, from_outer, from_inner)
        block = jnp.concatenate([low, block, high], axis=dim)
    return block


def window_matrix(local_bins, half_width):
    padded_index = jnp.arange(local_bins + 2 * half_width)[:, None]
    bin_index = jnp.arange(local_bins)[None, :]
    inside = (padded_index >= bin_index) & (padded_index <= bin_index + 2 * half_width)
    return inside.astype(jnp.bfloat16)


def exact_dot(values, selector):
    high = lax.reduce_precision(values, exponent_bits=8, mantissa_bits=7)
    rest = values - high
    mid = lax.reduce_precision(rest, exponent_bits=8, mantissa_bits=7)
    low = rest - mid
    total = jnp.dot(high.astype(jnp.bfloat16), selector, preferred_element_type=jnp.float32)
    total = total + jnp.dot(mid.astype(jnp.bfloat16), selector, preferred_element_type=jnp.float32)
    return total + jnp.dot(low.astype(jnp.bfloat16), selector, preferred_element_type=jnp.float32)


def select_rows(table, index):
    chosen = (index[:, None] == jnp.arange(table.shape[0], dtype=jnp.int32)[None, :]).astype(
        table.dtype
    )
    return jnp.dot(chosen, table, preferred_element_type=jnp.float32)


def lag_table(first_bin, local_bins, total_bins, lag_count):
    frequency = first_bin + jnp.arange(local_bins, dtype=jnp.int32)
    lag_index = jnp.arange(lag_count, dtype=jnp.int32) - lag_count // 2
    residue = frequency[:, None] * lag_index[None, :] % (2 * total_bins)
    angles = residue.astype(jnp.float32) * (math.pi / total_bins)
    cosine = jnp.cos(angles) / total_bins
    negsine = -jnp.sin(angles) / total_bins
    return jnp.concatenate([cosine, negsine], axis=0).astype(jnp.bfloat16)


def per_device(spectra, pair_first, pair_second, pair_bin):
    seg_position = lax.axis_index("seg")
    band_position = lax.axis_index("band")
    segments = lax.axis_size("seg")
    bands = lax.axis_size("band")
    channels = spectra.shape[1]
    local_bins = spectra.shape[2]
    real_part = spectra[0].astype(jnp.float32)
    imag_part = spectra[1].astype(jnp.float32)
    power_sum = real_part * real_part + imag_part * imag_part
    padded_power = extended(power_sum, (("band", 1),), HALF_WIN, jnp.bfloat16)
    table = lag_table(band_position * local_bins, local_bins, FREQ, LAGS)
    padded_power, table = lax.optimization_barrier((padded_power, table))
    window_sum = exact_dot(padded_power, window_matrix(local_bins, HALF_WIN))
    scaling = lax.rsqrt(window_sum / (2 * HALF_WIN + 1) + epsilon)
    whitened = jnp.concatenate([real_part * scaling, imag_part * scaling], axis=1).astype(
        jnp.bfloat16
    )
    first_rows = select_rows(whitened, pair_first - seg_position * channels)
    near_rows = extended(whitened, (("seg", 0),), REACH)
    second_rows = select_rows(near_rows, pair_second - seg_position * channels + REACH)
    first_real = first_rows[:, :local_bins]
    first_imag = first_rows[:, local_bins:]
    second_real = second_rows[:, :local_bins]
    second_imag = second_rows[:, local_bins:]
    cross_real = first_real * second_real + first_imag * second_imag
    cross_imag = first_imag * second_real - first_real * second_imag
    all_bins = segments * OB_DEV
    members = (pair_bin[:, None] == jnp.arange(all_bins, dtype=jnp.int32)[None, :]).astype(
        jnp.bfloat16
    )
    by_bin = (((0,), (0,)), ((), ()))
    stack_real = lax.dot_general(
        members, cross_real.astype(jnp.bfloat16), by_bin, preferred_element_type=jnp.float32
    )
    stack_imag = lax.dot_general(
        members, cross_imag.astype(jnp.bfloat16), by_bin, preferred_element_type=jnp.float32
    )
    local_stack = jnp.concatenate([stack_real, stack_imag], axis=1)
    gathered = lax.all_to_all(
        local_stack.astype(jnp.bfloat16), "seg", split_axis=0, concat_axis=0, tiled=True
    )
    stack = jnp.sum(
        gathered.reshape(segments, OB_DEV, 2 * local_bins).astype(jnp.float32), axis=0
    )
    partial_lags = jnp.dot(
        stack, table.astype(jnp.float32), precision=lax.Precision.HIGHEST
    )
    pieces = lax.all_to_all(partial_lags, "band", split_axis=1, concat_axis=0, tiled=True)
    return jnp.sum(pieces.reshape(bands, OB_DEV, LAGS // bands), axis=0)


def solution(mesh):
    placed = (P(None, "seg", "band"), P("seg"), P("seg"), P("seg"))
    return jax.shard_map(
        per_device, mesh=mesh, in_specs=placed, out_specs=P("seg", "band"), check_vma=False
    )
```

```python
import math

import jax
import jax.numpy as jnp
from jax import lax
from jax.sharding import PartitionSpec as P

OB_DEV = 8
REACH = 256
FREQ = 1024
LAGS = 1024
HALF_WIN = 64


epsilon = 1e-06


def extended(block, sides, width, wire=None):
    for axis, dim in sides:
        count = lax.axis_size(axis)
        odd = lax.axis_index(axis) % 2 == 1
        first = lax.slice_in_dim(block, 0, width, axis=dim)
        last = lax.slice_in_dim(block, block.shape[dim] - width, None, axis=dim)
        inner = [(i, i ^ 1) for i in range(count - count % 2)]
        outer = [(i, i + 1) for i in range(1, count - 1, 2)]
        outer = outer + [(target, source) for source, target in outer]
        wire_type = block.dtype if wire is None else wire
        from_inner = lax.ppermute(jnp.where(odd, first, last).astype(wire_type), axis, inner)
        from_outer = lax.ppermute(jnp.where(odd, last, first).astype(wire_type), axis, outer)
        from_inner = from_inner.astype(block.dtype)
        from_outer = from_outer.astype(block.dtype)
        low = jnp.where(odd, from_inner, from_outer)
        high = jnp.where(odd, from_outer, from_inner)
        block = jnp.concatenate([low, block, high], axis=dim)
    return block


def window_matrix(local_bins, half_width):
    padded_index = jnp.arange(local_bins + 2 * half_width)[:, None]
    bin_index = jnp.arange(local_bins)[None, :]
    inside = (padded_index >= bin_index) & (padded_index <= bin_index + 2 * half_width)
    return inside.astype(jnp.bfloat16)


def exact_dot(values, selector):
    high = lax.reduce_precision(values, exponent_bits=8, mantissa_bits=7)
    rest = values - high
    mid = lax.reduce_precision(rest, exponent_bits=8, mantissa_bits=7)
    low = rest - mid
    total = jnp.dot(high.astype(jnp.bfloat16), selector, preferred_element_type=jnp.float32)
    total = total + jnp.dot(mid.astype(jnp.bfloat16), selector, preferred_element_type=jnp.float32)
    return total + jnp.dot(low.astype(jnp.bfloat16), selector, preferred_element_type=jnp.float32)


def select_rows(table, index):
    chosen = (index[:, None] == jnp.arange(table.shape[0], dtype=jnp.int32)[None, :]).astype(
        table.dtype
    )
    return jnp.dot(chosen, table, preferred_element_type=jnp.float32).astype(table.dtype)


def lag_table(first_bin, local_bins, total_bins, lag_count):
    frequency = first_bin + jnp.arange(local_bins, dtype=jnp.int32)
    lag_index = jnp.arange(lag_count, dtype=jnp.int32) - lag_count // 2
    residue = frequency[:, None] * lag_index[None, :] % (2 * total_bins)
    angles = residue.astype(jnp.float32) * (math.pi / total_bins)
    cosine = jnp.cos(angles) / total_bins
    negsine = -jnp.sin(angles) / total_bins
    return jnp.concatenate([cosine, negsine], axis=0).astype(jnp.bfloat16)


def per_device(spectra, pair_first, pair_second, pair_bin):
    seg_position = lax.axis_index("seg")
    band_position = lax.axis_index("band")
    segments = lax.axis_size("seg")
    bands = lax.axis_size("band")
    channels = spectra.shape[1]
    local_bins = spectra.shape[2]
    real_part = spectra[0].astype(jnp.float32)
    imag_part = spectra[1].astype(jnp.float32)
    power_sum = real_part * real_part + imag_part * imag_part
    padded_power = extended(power_sum, (("band", 1),), HALF_WIN, jnp.bfloat16)
    table = lag_table(band_position * local_bins, local_bins, FREQ, LAGS)
    padded_power, table = lax.optimization_barrier((padded_power, table))
    window_sum = exact_dot(padded_power, window_matrix(local_bins, HALF_WIN))
    scaling = lax.rsqrt(window_sum / (2 * HALF_WIN + 1) + epsilon)
    whitened = jnp.concatenate([real_part * scaling, imag_part * scaling], axis=1).astype(
        jnp.bfloat16
    )
    first_rows = select_rows(whitened, pair_first - seg_position * channels)
    near_rows = extended(whitened, (("seg", 0),), REACH)
    second_rows = select_rows(near_rows, pair_second - seg_position * channels + REACH)
    first_real = first_rows[:, :local_bins].astype(jnp.float32)
    first_imag = first_rows[:, local_bins:].astype(jnp.float32)
    second_real = second_rows[:, :local_bins].astype(jnp.float32)
    second_imag = second_rows[:, local_bins:].astype(jnp.float32)
    cross_real = first_real * second_real + first_imag * second_imag
    cross_imag = first_imag * second_real - first_real * second_imag
    cross_both = jnp.concatenate([cross_real, cross_imag], axis=1).astype(jnp.bfloat16)
    all_bins = segments * OB_DEV
    members = (pair_bin[:, None] == jnp.arange(all_bins, dtype=jnp.int32)[None, :]).astype(
        jnp.bfloat16
    )
    local_stack = lax.dot_general(
        members, cross_both, (((0,), (0,)), ((), ())), preferred_element_type=jnp.float32
    )
    gathered = lax.all_to_all(
        local_stack.astype(jnp.bfloat16), "seg", split_axis=0, concat_axis=0, tiled=True
    )
    stack = jnp.sum(
        gathered.reshape(segments, OB_DEV, 2 * local_bins).astype(jnp.float32), axis=0
    )
    partial_lags = jnp.dot(
        stack, table.astype(jnp.float32), precision=lax.Precision.HIGHEST
    )
    pieces = lax.all_to_all(partial_lags, "band", split_axis=1, concat_axis=0, tiled=True)
    return jnp.sum(pieces.reshape(bands, OB_DEV, LAGS // bands), axis=0)


def solution(mesh):
    placed = (P(None, "seg", "band"), P("seg"), P("seg"), P("seg"))
    return jax.shard_map(
        per_device, mesh=mesh, in_specs=placed, out_specs=P("seg", "band"), check_vma=False
    )
```

```python
import math

import jax
import jax.numpy as jnp
from jax import lax
from jax.sharding import PartitionSpec as P

OB_DEV = 8
REACH = 256
FREQ = 1024
LAGS = 1024
HALF_WIN = 64


epsilon = 1e-06


def extended(block, sides, width, wire=None):
    for axis, dim in sides:
        count = lax.axis_size(axis)
        odd = lax.axis_index(axis) % 2 == 1
        first = lax.slice_in_dim(block, 0, width, axis=dim)
        last = lax.slice_in_dim(block, block.shape[dim] - width, None, axis=dim)
        inner = [(i, i ^ 1) for i in range(count - count % 2)]
        outer = [(i, i + 1) for i in range(1, count - 1, 2)]
        outer = outer + [(target, source) for source, target in outer]
        wire_type = block.dtype if wire is None else wire
        from_inner = lax.ppermute(jnp.where(odd, first, last).astype(wire_type), axis, inner)
        from_outer = lax.ppermute(jnp.where(odd, last, first).astype(wire_type), axis, outer)
        from_inner = from_inner.astype(block.dtype)
        from_outer = from_outer.astype(block.dtype)
        low = jnp.where(odd, from_inner, from_outer)
        high = jnp.where(odd, from_outer, from_inner)
        block = jnp.concatenate([low, block, high], axis=dim)
    return block


def window_matrix(local_bins, half_width):
    padded_index = jnp.arange(local_bins + 2 * half_width)[:, None]
    bin_index = jnp.arange(local_bins)[None, :]
    inside = (padded_index >= bin_index) & (padded_index <= bin_index + 2 * half_width)
    return inside.astype(jnp.bfloat16)


def exact_dot(values, selector):
    high = lax.reduce_precision(values, exponent_bits=8, mantissa_bits=7)
    rest = values - high
    mid = lax.reduce_precision(rest, exponent_bits=8, mantissa_bits=7)
    low = rest - mid
    total = jnp.dot(high.astype(jnp.bfloat16), selector, preferred_element_type=jnp.float32)
    total = total + jnp.dot(mid.astype(jnp.bfloat16), selector, preferred_element_type=jnp.float32)
    return total + jnp.dot(low.astype(jnp.bfloat16), selector, preferred_element_type=jnp.float32)


def select_rows(table, index):
    chosen = (index[:, None] == jnp.arange(table.shape[0], dtype=jnp.int32)[None, :]).astype(
        table.dtype
    )
    return jnp.dot(chosen, table, preferred_element_type=jnp.float32)


def lag_table(first_bin, local_bins, total_bins, lag_count):
    frequency = first_bin + jnp.arange(local_bins, dtype=jnp.int32)
    lag_index = jnp.arange(lag_count, dtype=jnp.int32) - lag_count // 2
    residue = frequency[:, None] * lag_index[None, :] % (2 * total_bins)
    angles = residue.astype(jnp.float32) * (math.pi / total_bins)
    cosine = jnp.cos(angles) / total_bins
    negsine = -jnp.sin(angles) / total_bins
    return jnp.concatenate([cosine, negsine], axis=0).astype(jnp.bfloat16)


def per_device(spectra, pair_first, pair_second, pair_bin):
    seg_position = lax.axis_index("seg")
    band_position = lax.axis_index("band")
    segments = lax.axis_size("seg")
    bands = lax.axis_size("band")
    channels = spectra.shape[1]
    local_bins = spectra.shape[2]
    real_part = spectra[0].astype(jnp.float32)
    imag_part = spectra[1].astype(jnp.float32)
    power_sum = real_part * real_part + imag_part * imag_part
    padded_power = extended(power_sum, (("band", 1),), HALF_WIN, jnp.bfloat16)
    table = lag_table(band_position * local_bins, local_bins, FREQ, LAGS)
    padded_power, table = lax.optimization_barrier((padded_power, table))
    window_sum = exact_dot(padded_power, window_matrix(local_bins, HALF_WIN))
    scaling = lax.rsqrt(window_sum / (2 * HALF_WIN + 1) + epsilon)
    whitened = jnp.concatenate([real_part * scaling, imag_part * scaling], axis=1).astype(
        jnp.bfloat16
    )
    first_rows = select_rows(whitened, pair_first - seg_position * channels)
    near_rows = extended(whitened, (("seg", 0),), REACH)
    second_rows = select_rows(near_rows, pair_second - seg_position * channels + REACH)
    first_real = first_rows[:, :local_bins]
    first_imag = first_rows[:, local_bins:]
    second_real = second_rows[:, :local_bins]
    second_imag = second_rows[:, local_bins:]
    cross_real = first_real * second_real + first_imag * second_imag
    cross_imag = first_imag * second_real - first_real * second_imag
    cross_both = jnp.concatenate([cross_real, cross_imag], axis=1).astype(jnp.bfloat16)
    all_bins = segments * OB_DEV
    members = (pair_bin[:, None] == jnp.arange(all_bins, dtype=jnp.int32)[None, :]).astype(
        jnp.bfloat16
    )
    local_stack = lax.dot_general(
        members, cross_both, (((0,), (0,)), ((), ())), preferred_element_type=jnp.float32
    )
    gathered = lax.all_to_all(
        local_stack.astype(jnp.bfloat16), "seg", split_axis=0, concat_axis=0, tiled=True
    )
    stack = jnp.sum(
        gathered.reshape(segments, OB_DEV, 2 * local_bins).astype(jnp.float32), axis=0
    )
    partial_lags = jnp.dot(
        stack, table.astype(jnp.float32), precision=lax.Precision.HIGHEST
    )
    pieces = lax.all_to_all(
        partial_lags.astype(jnp.bfloat16), "band", split_axis=1, concat_axis=0, tiled=True
    )
    return jnp.sum(pieces.reshape(bands, OB_DEV, LAGS // bands).astype(jnp.float32), axis=0)


def solution(mesh):
    placed = (P(None, "seg", "band"), P("seg"), P("seg"), P("seg"))
    return jax.shard_map(
        per_device, mesh=mesh, in_specs=placed, out_specs=P("seg", "band"), check_vma=False
    )
```

```python
import math

import jax
import jax.numpy as jnp
from jax import lax
from jax.sharding import PartitionSpec as P

OB_DEV = 8
REACH = 256
FREQ = 1024
LAGS = 1024
HALF_WIN = 64


epsilon = 1e-06


def extended(block, sides, width, wire=None):
    for axis, dim in sides:
        count = lax.axis_size(axis)
        odd = lax.axis_index(axis) % 2 == 1
        first = lax.slice_in_dim(block, 0, width, axis=dim)
        last = lax.slice_in_dim(block, block.shape[dim] - width, None, axis=dim)
        inner = [(i, i ^ 1) for i in range(count - count % 2)]
        outer = [(i, i + 1) for i in range(1, count - 1, 2)]
        outer = outer + [(target, source) for source, target in outer]
        wire_type = block.dtype if wire is None else wire
        from_inner = lax.ppermute(jnp.where(odd, first, last).astype(wire_type), axis, inner)
        from_outer = lax.ppermute(jnp.where(odd, last, first).astype(wire_type), axis, outer)
        from_inner = from_inner.astype(block.dtype)
        from_outer = from_outer.astype(block.dtype)
        low = jnp.where(odd, from_inner, from_outer)
        high = jnp.where(odd, from_outer, from_inner)
        block = jnp.concatenate([low, block, high], axis=dim)
    return block


def window_matrix(local_bins, half_width):
    padded_index = jnp.arange(local_bins + 2 * half_width)[:, None]
    bin_index = jnp.arange(local_bins)[None, :]
    inside = (padded_index >= bin_index) & (padded_index <= bin_index + 2 * half_width)
    return inside.astype(jnp.bfloat16)


def exact_dot(values, selector):
    high = lax.reduce_precision(values, exponent_bits=8, mantissa_bits=7)
    rest = values - high
    total = jnp.dot(high.astype(jnp.bfloat16), selector, preferred_element_type=jnp.float32)
    return total + jnp.dot(rest.astype(jnp.bfloat16), selector, preferred_element_type=jnp.float32)


def select_rows(table, index):
    chosen = (index[:, None] == jnp.arange(table.shape[0], dtype=jnp.int32)[None, :]).astype(
        table.dtype
    )
    return jnp.dot(chosen, table, preferred_element_type=jnp.float32)


def lag_table(first_bin, local_bins, total_bins, lag_count):
    frequency = first_bin + jnp.arange(local_bins, dtype=jnp.int32)
    lag_index = jnp.arange(lag_count, dtype=jnp.int32) - lag_count // 2
    residue = frequency[:, None] * lag_index[None, :] % (2 * total_bins)
    angles = residue.astype(jnp.float32) * (math.pi / total_bins)
    cosine = jnp.cos(angles) / total_bins
    negsine = -jnp.sin(angles) / total_bins
    return jnp.concatenate([cosine, negsine], axis=0).astype(jnp.bfloat16)


def per_device(spectra, pair_first, pair_second, pair_bin):
    seg_position = lax.axis_index("seg")
    band_position = lax.axis_index("band")
    segments = lax.axis_size("seg")
    bands = lax.axis_size("band")
    channels = spectra.shape[1]
    local_bins = spectra.shape[2]
    real_part = spectra[0].astype(jnp.float32)
    imag_part = spectra[1].astype(jnp.float32)
    power_sum = real_part * real_part + imag_part * imag_part
    padded_power = extended(power_sum, (("band", 1),), HALF_WIN, jnp.bfloat16)
    table = lag_table(band_position * local_bins, local_bins, FREQ, LAGS)
    padded_power, table = lax.optimization_barrier((padded_power, table))
    window_sum = exact_dot(padded_power, window_matrix(local_bins, HALF_WIN))
    scaling = lax.rsqrt(window_sum / (2 * HALF_WIN + 1) + epsilon)
    whitened = jnp.concatenate([real_part * scaling, imag_part * scaling], axis=1).astype(
        jnp.bfloat16
    )
    first_rows = select_rows(whitened, pair_first - seg_position * channels)
    near_rows = extended(whitened, (("seg", 0),), REACH)
    second_rows = select_rows(near_rows, pair_second - seg_position * channels + REACH)
    first_real = first_rows[:, :local_bins]
    first_imag = first_rows[:, local_bins:]
    second_real = second_rows[:, :local_bins]
    second_imag = second_rows[:, local_bins:]
    cross_real = first_real * second_real + first_imag * second_imag
    cross_imag = first_imag * second_real - first_real * second_imag
    cross_both = jnp.concatenate([cross_real, cross_imag], axis=1).astype(jnp.bfloat16)
    all_bins = segments * OB_DEV
    members = (pair_bin[:, None] == jnp.arange(all_bins, dtype=jnp.int32)[None, :]).astype(
        jnp.bfloat16
    )
    local_stack = lax.dot_general(
        members, cross_both, (((0,), (0,)), ((), ())), preferred_element_type=jnp.float32
    )
    gathered = lax.all_to_all(
        local_stack.astype(jnp.bfloat16), "seg", split_axis=0, concat_axis=0, tiled=True
    )
    stack = jnp.sum(
        gathered.reshape(segments, OB_DEV, 2 * local_bins).astype(jnp.float32), axis=0
    )
    partial_lags = jnp.dot(
        stack, table.astype(jnp.float32), precision=lax.Precision.HIGHEST
    )
    pieces = lax.all_to_all(partial_lags, "band", split_axis=1, concat_axis=0, tiled=True)
    return jnp.sum(pieces.reshape(bands, OB_DEV, LAGS // bands), axis=0)


def solution(mesh):
    placed = (P(None, "seg", "band"), P("seg"), P("seg"), P("seg"))
    return jax.shard_map(
        per_device, mesh=mesh, in_specs=placed, out_specs=P("seg", "band"), check_vma=False
    )
```
